256 devices in a mesh: dom: 32 (over y, x, core), rot: 8 (over z).
Axes of the slice: x: 4, y: 4, z: 8, core: 2. Of those that a mesh axis runs over, the one named last changes fastest.
Arguments:
- particles: bfloat16 [2048, 8192], P('dom'), may hold values from -8 to 8, as said below
- assign: int32 [2048], P('dom'), may hold values from 0 to 191, as said below
- rot_index: int32 [2048], P('dom'), may hold values from 0 to 63
- group: int32 [2048], P('dom'), may hold values from 0 to 31
- ctf_table: float32 [32, 64], replicated, may hold values from -1 to 1
Outputs:
- refs: bfloat16 [192, 8192], P('dom')
- best_scores: float32 [2048, 192], P(('dom', 'rot'))
The draws below stay inside these ranges and needn't reach their ends.
Inputs may be any that keep to these rules, and one draw needn't show every extreme that they name: `particles`: rows in custom order; values real. `assign`: owner o holds classes o * 6 to o * 6 + 5. The 64 particles of one index of dom form 8 shares of 8 consecutive particles; within each share at most 2 particles are assigned to the classes of one owner.
All inputs are finite; a program needn't handle non-finite values.
Results may differ from the reference program's by a relative error of at most 0.0027.
Values may be sent and summed in bfloat16 or wider, within the bound.
No kernel may reach another device: no remote copies, remote signals or barrier semaphores. Data moves between devices by JAX's collectives and lax.ppermute only.
A program may use at most 128 MiB of HBM per device.

```python
import math
import jax
import jax.numpy as jnp
from jax import lax

CYCLES = 64
MFREQ = 64
CLS_DEV = 6
GROUPS = 32
P_DEV = 64
K = 8192
CLASSES = 192
ROT = 64
PARTICLES = 2048
SHARE = 8
CAP = 2
N_DOM = 32
N_ROT = 8


def draw_particles(key, part):
    base_key = jax.random.fold_in(key, 7)
    key_column, key_values = jax.random.split(base_key, 2)
    column = jnp.exp(jax.random.uniform(key_column, (K,), jnp.float32, 0.0, math.log(10.0))) / math.sqrt(10.0)
    values = jax.random.normal(key_values, (PARTICLES, K), jnp.float32) * column[None, :]
    return jnp.clip(values, -8.0, 8.0).astype(jnp.bfloat16)


def shuffled_slots(one_key):
    return jax.random.permutation(one_key, (N_DOM - 1) * (CAP - 1))


def shuffled_rows(one_key):
    return jax.random.permutation(one_key, SHARE)


def draw_assign(key, part):
    base_key = jax.random.fold_in(key, 13)
    key_hot, key_slots, key_order, key_within = jax.random.split(base_key, 4)
    blocks = PARTICLES // SHARE
    hot = jax.random.randint(key_hot, (N_ROT,), 0, N_DOM)
    hot_rows = hot[jnp.arange(blocks) % N_ROT]
    picks = jax.vmap(shuffled_slots)(jax.random.split(key_slots, blocks))[:, :SHARE - CAP]
    others = (hot_rows[:, None] + 1 + picks // (CAP - 1)) % N_DOM
    owners = jnp.concatenate([jnp.broadcast_to(hot_rows[:, None], (blocks, CAP)), others], axis=1)
    order = jax.vmap(shuffled_rows)(jax.random.split(key_order, blocks))
    owners = jnp.take_along_axis(owners, order, axis=1)
    within = jax.random.randint(key_within, (blocks, SHARE), 0, CLS_DEV)
    return (owners * CLS_DEV + within).reshape(PARTICLES).astype(jnp.int32)


def plant(result, own_key, low, largest):
    longest = result.shape.index(max(result.shape))
    spots = []
    for shift in (0, 1):
        where = [jax.random.randint(jax.random.fold_in(own_key, axis), (), 0, length) for axis, length in enumerate(result.shape)]
        where[longest] = (where[longest] + shift) % result.shape[longest]
        spots.append(tuple(where))
    return result.at[spots[0]].set(low).at[spots[1]].set(largest)


def setup_inputs(seed: int = 0) -> dict:
    keys = jax.random.split(jax.random.key(seed), 6)
    return {
        "particles": draw_particles(jax.random.fold_in(keys[5], 71), 0),
        "assign": draw_assign(jax.random.fold_in(keys[5], 71), 0),
        "rot_index": plant(jax.random.randint(keys[2], (PARTICLES,), 0, ROT), jax.random.fold_in(keys[2], 1), 0, ROT - 1).astype(jnp.int32),
        "group": plant(jax.random.randint(keys[3], (PARTICLES,), 0, GROUPS), jax.random.fold_in(keys[3], 1), 0, GROUPS - 1).astype(jnp.int32),
        "ctf_table": jnp.clip(jax.random.uniform(keys[4], (GROUPS, CYCLES), jnp.float32, -1.0, 1.0), -1.0, 1.0),
    }


def angles(index, total):
    freqs = jnp.arange(MFREQ, dtype=jnp.int32)
    phase = freqs[None, :] * index[:, None] % total
    return phase.astype(jnp.float32) * (2.0 * math.pi / total)

def derotate(spec, rotation, ctf_rows, total):
    count = spec.shape[0]
    layered = spec.reshape(count, 2, CYCLES, MFREQ)
    real_part = layered[:, 0]
    imag_part = layered[:, 1]
    angle = angles(rotation, total)
    cosine = jnp.cos(angle)[:, None, :]
    sine = jnp.sin(angle)[:, None, :]
    turned = jnp.stack([real_part * cosine + imag_part * sine, imag_part * cosine - real_part * sine], axis=1)
    return (turned * ctf_rows[:, None, :, None]).reshape(count, K)

def rotate_refs(refs, rotation, total):
    count = refs.shape[0]
    layered = refs.astype(jnp.float32).reshape(count, 2, CYCLES, MFREQ)
    real_part = layered[:, 0]
    imag_part = layered[:, 1]
    angle = angles(jnp.reshape(rotation, (1,)).astype(jnp.int32), total)
    cosine = jnp.cos(angle)
    sine = jnp.sin(angle)
    turned = jnp.stack([real_part * cosine - imag_part * sine, real_part * sine + imag_part * cosine], axis=1)
    return turned.reshape(count, K).astype(jnp.bfloat16)

def reference(particles, assign, rot_index, group, ctf_table):
    ctf_rows = ctf_table[group]

    def absorb(carry, block_index):
        numer, denom = carry
        first = (block_index * P_DEV).astype(jnp.int32)
        rows = lax.dynamic_slice_in_dim(particles, first, P_DEV, 0).astype(jnp.float32)
        labels = lax.dynamic_slice_in_dim(assign, first, P_DEV, 0)
        turns = lax.dynamic_slice_in_dim(rot_index, first, P_DEV, 0)
        factors = lax.dynamic_slice_in_dim(ctf_rows, first, P_DEV, 0)
        weighted = derotate(rows, turns, factors, ROT)
        numer = numer + jax.ops.segment_sum(weighted, labels, num_segments=CLASSES)
        denom = denom + jax.ops.segment_sum(factors * factors, labels, num_segments=CLASSES)
        return ((numer, denom), None)
    start_carry = (jnp.zeros((CLASSES, K), jnp.float32), jnp.zeros((CLASSES, CYCLES), jnp.float32))
    (numer, denom), _ = lax.scan(absorb, start_carry, jnp.arange(PARTICLES // P_DEV, dtype=jnp.int32))
    plain = numer.reshape(CLASSES, 2, CYCLES, MFREQ) / (denom[:, None, :, None] + 1.0)
    spread = lax.optimization_barrier(jnp.mean(plain * plain, axis=(1, 2, 3)))
    refs = (plain / jnp.sqrt(spread + 1e-06)[:, None, None, None]).reshape(CLASSES, K).astype(jnp.bfloat16)
    modulated = (particles.astype(jnp.float32).reshape(PARTICLES, 2, CYCLES, MFREQ) * ctf_rows[:, None, :, None]).reshape(PARTICLES, K).astype(jnp.bfloat16)
    widened = modulated.astype(jnp.float32)
    scale = 1.0 / math.sqrt(K)

    def score(best, rotation):
        turned = rotate_refs(refs, rotation, ROT).astype(jnp.float32)
        found = jnp.dot(widened, turned.T, preferred_element_type=jnp.float32) * scale
        return (jnp.maximum(best, found), None)
    start_best = jnp.full((PARTICLES, CLASSES), -jnp.inf, jnp.float32)
    best_scores, _ = lax.scan(score, start_best, jnp.arange(ROT, dtype=jnp.int32))
    return (refs, best_scores)
```

```python
import math

import jax
import jax.numpy as jnp
from jax import lax
from jax.sharding import PartitionSpec as P

CYCLES = 64
MFREQ = 64
CLS_DEV = 6
K = 8192


def angles(index, total):
    freqs = jnp.arange(MFREQ, dtype=jnp.int32)
    phase = freqs[None, :] * index[:, None] % total
    return phase.astype(jnp.float32) * (2.0 * math.pi / total)


def derotate(spec, rotation, ctf_rows, total):
    count = spec.shape[0]
    layered = spec.reshape(count, 2, CYCLES, MFREQ)
    real_part = layered[:, 0]
    imag_part = layered[:, 1]
    angle = angles(rotation, total)
    cosine = jnp.cos(angle)[:, None, :]
    sine = jnp.sin(angle)[:, None, :]
    turned = jnp.stack(
        [real_part * cosine + imag_part * sine, imag_part * cosine - real_part * sine], axis=1
    )
    return (turned * ctf_rows[:, None, :, None]).reshape(count, K)


def rotate_all(refs, total):
    count = refs.shape[0]
    layered = refs.astype(jnp.float32).reshape(count, 2, CYCLES, MFREQ)
    real_part = layered[None, :, 0]
    imag_part = layered[None, :, 1]
    angle = angles(jnp.arange(total, dtype=jnp.int32), total)
    cosine = jnp.cos(angle)[:, None, None, :]
    sine = jnp.sin(angle)[:, None, None, :]
    turned = jnp.stack(
        [real_part * cosine - imag_part * sine, real_part * sine + imag_part * cosine], axis=2
    )
    return turned.reshape(total * count, K).astype(jnp.bfloat16)


def local(particles, assign, rot_index, group, ctf_table):
    dom_rank = lax.axis_index("dom")
    rot_count = lax.axis_size("rot")
    rot_rank = lax.axis_index("rot")
    dom_count = lax.axis_size("dom")
    classes = CLS_DEV * dom_count
    block = classes // rot_count
    owners_per_block = block // CLS_DEV
    total = 8 * rot_count
    count = particles.shape[0]

    ctf_rows = ctf_table[group]
    spec = particles.astype(jnp.float32)
    weighted = derotate(spec, rot_index, ctf_rows, total)
    first_class = rot_rank * block
    member = (
        (first_class + jnp.arange(block, dtype=jnp.int32))[:, None] == assign[None, :]
    ).astype(jnp.float32)
    numer = jnp.dot(
        member, weighted, precision=lax.Precision.HIGHEST, preferred_element_type=jnp.float32
    )
    denom = jnp.dot(
        member,
        ctf_rows * ctf_rows,
        precision=lax.Precision.HIGHEST,
        preferred_element_type=jnp.float32,
    )
    numer, denom = lax.psum((numer, denom), "dom")
    plain = numer.reshape(block, 2, CYCLES, MFREQ) / (denom[:, None, :, None] + 1.0)
    spread = jnp.mean(plain * plain, axis=(1, 2, 3))
    refs_block = (
        (plain / jnp.sqrt(spread + 1e-06)[:, None, None, None])
        .reshape(block, K)
        .astype(jnp.bfloat16)
    )

    modulated = (
        (spec.reshape(count, 2, CYCLES, MFREQ) * ctf_rows[:, None, :, None])
        .reshape(count, K)
        .astype(jnp.bfloat16)
    )
    turned = rotate_all(refs_block, total)
    found = lax.dot_general(
        modulated, turned, (((1,), (1,)), ((), ())), preferred_element_type=jnp.float32
    )
    best = jnp.max(found.reshape(count, total, block), axis=1) * (1.0 / math.sqrt(K))
    best_scores = lax.all_to_all(best, "rot", 0, 1, tiled=True)

    mine = lax.dynamic_slice_in_dim(refs_block, (dom_rank % owners_per_block) * CLS_DEV, CLS_DEV, 0)
    keep = (dom_rank // owners_per_block) == rot_rank
    refs = lax.psum(jnp.where(keep, mine, jnp.zeros_like(mine)), "rot")
    return (refs, best_scores)


def solution(mesh):
    in_specs = (P("dom", None), P("dom"), P("dom"), P("dom"), P())
    out_specs = (P("dom", None), P(("dom", "rot"), None))
    return jax.shard_map(local, mesh=mesh, in_specs=in_specs, out_specs=out_specs, check_vma=False)
```

```python
import math

import jax
import jax.numpy as jnp
from jax import lax
from jax.sharding import PartitionSpec as P

CYCLES = 64
MFREQ = 64
CLS_DEV = 6
K = 8192


def angles(index, total):
    freqs = jnp.arange(MFREQ, dtype=jnp.int32)
    phase = freqs[None, :] * index[:, None] % total
    return phase.astype(jnp.float32) * (2.0 * math.pi / total)


def derotate(spec, rotation, ctf_rows, total):
    count = spec.shape[0]
    layered = spec.reshape(count, 2, CYCLES, MFREQ)
    real_part = layered[:, 0]
    imag_part = layered[:, 1]
    angle = angles(rotation, total)
    cosine = jnp.cos(angle)[:, None, :]
    sine = jnp.sin(angle)[:, None, :]
    turned = jnp.stack(
        [real_part * cosine + imag_part * sine, imag_part * cosine - real_part * sine], axis=1
    )
    return (turned * ctf_rows[:, None, :, None]).reshape(count, K)


def rotate_all(refs, total):
    count = refs.shape[0]
    half = K // 2
    real_part = refs[None, :, :half]
    imag_part = refs[None, :, half:]
    angle = angles(jnp.arange(total, dtype=jnp.int32), total)
    cosine = jnp.tile(jnp.cos(angle), (1, CYCLES))[:, None, :]
    sine = jnp.tile(jnp.sin(angle), (1, CYCLES))[:, None, :]
    turned = jnp.concatenate(
        [real_part * cosine - imag_part * sine, real_part * sine + imag_part * cosine], axis=2
    )
    return turned.reshape(total * count, K).astype(jnp.bfloat16)


def local(particles, assign, rot_index, group, ctf_table):
    dom_rank = lax.axis_index("dom")
    rot_count = lax.axis_size("rot")
    rot_rank = lax.axis_index("rot")
    dom_count = lax.axis_size("dom")
    classes = CLS_DEV * dom_count
    block = classes // rot_count
    owners_per_block = block // CLS_DEV
    total = 8 * rot_count
    count = particles.shape[0]

    ctf_rows = ctf_table[group]
    spec = particles.astype(jnp.float32)
    weighted = derotate(spec, rot_index, ctf_rows, total)
    first_class = rot_rank * block
    member = (
        (first_class + jnp.arange(block, dtype=jnp.int32))[:, None] == assign[None, :]
    ).astype(jnp.float32)
    numer = jnp.dot(
        member, weighted, precision=lax.Precision.HIGHEST, preferred_element_type=jnp.float32
    )
    denom = jnp.dot(
        member,
        ctf_rows * ctf_rows,
        precision=lax.Precision.HIGHEST,
        preferred_element_type=jnp.float32,
    )
    chunks = dom_count
    width = K // chunks
    per_chunk = width // MFREQ
    payload = jnp.concatenate(
        [
            numer.reshape(block, chunks, width).transpose(1, 0, 2),
            jnp.broadcast_to(denom[None], (chunks, block, CYCLES)),
        ],
        axis=2,
    )
    summed = jnp.sum(lax.all_to_all(payload, "dom", 0, 0, tiled=True), axis=0)
    numer_chunk = summed[:, :width].reshape(block, per_chunk, MFREQ)
    first_cycle = (dom_rank * per_chunk) % CYCLES
    denom_chunk = lax.dynamic_slice_in_dim(summed[:, width:], first_cycle, per_chunk, 1)
    plain_chunk = (numer_chunk / (denom_chunk[:, :, None] + 1.0)).reshape(block, width)
    plain = lax.all_to_all(
        jnp.broadcast_to(plain_chunk[None], (chunks, block, width)), "dom", 0, 0, tiled=True
    )
    plain = plain.transpose(1, 0, 2).reshape(block, K)
    spread = jnp.mean(plain * plain, axis=1)
    refs_f32 = plain / jnp.sqrt(spread + 1e-06)[:, None]
    refs_block = refs_f32.astype(jnp.bfloat16)

    modulated = (
        (spec.reshape(count, 2, CYCLES, MFREQ) * ctf_rows[:, None, :, None])
        .reshape(count, K)
        .astype(jnp.bfloat16)
    )
    turned = rotate_all(refs_block.astype(jnp.float32), total)
    found = lax.dot_general(
        modulated, turned, (((1,), (1,)), ((), ())), preferred_element_type=jnp.float32
    )
    best = jnp.max(found.reshape(count, total, block), axis=1) * (1.0 / math.sqrt(K))
    best_scores = lax.all_to_all(best, "rot", 0, 1, tiled=True)

    mine = lax.dynamic_slice_in_dim(refs_block, (dom_rank % owners_per_block) * CLS_DEV, CLS_DEV, 0)
    spread_out = lax.all_to_all(
        jnp.broadcast_to(mine[None], (rot_count,) + mine.shape), "rot", 0, 0, tiled=True
    )
    refs = lax.dynamic_index_in_dim(spread_out, dom_rank // owners_per_block, 0, keepdims=False)
    return (refs, best_scores)


def solution(mesh):
    in_specs = (P("dom", None), P("dom"), P("dom"), P("dom"), P())
    out_specs = (P("dom", None), P(("dom", "rot"), None))
    return jax.shard_map(local, mesh=mesh, in_specs=in_specs, out_specs=out_specs, check_vma=False)
```

```python
import math

import jax
import jax.numpy as jnp
from jax import lax
from jax.sharding import PartitionSpec as P

CYCLES = 64
MFREQ = 64
CLS_DEV = 6
K = 8192


def angles(index, total):
    freqs = jnp.arange(MFREQ, dtype=jnp.int32)
    phase = freqs[None, :] * index[:, None] % total
    return phase.astype(jnp.float32) * (2.0 * math.pi / total)


def derotate(real_part, imag_part, rotation, ctf_cols, total):
    angle = angles(rotation, total)
    cosine = jnp.tile(jnp.cos(angle), (1, CYCLES))
    sine = jnp.tile(jnp.sin(angle), (1, CYCLES))
    return jnp.concatenate(
        [
            (real_part * cosine + imag_part * sine) * ctf_cols,
            (imag_part * cosine - real_part * sine) * ctf_cols,
        ],
        axis=1,
    )


def rotate_all(refs, total):
    count = refs.shape[0]
    half = K // 2
    real_part = refs[None, :, :half]
    imag_part = refs[None, :, half:]
    angle = angles(jnp.arange(total, dtype=jnp.int32), total)
    cosine = jnp.tile(jnp.cos(angle), (1, CYCLES))[:, None, :]
    sine = jnp.tile(jnp.sin(angle), (1, CYCLES))[:, None, :]
    turned = jnp.concatenate(
        [real_part * cosine - imag_part * sine, real_part * sine + imag_part * cosine], axis=2
    )
    return turned.reshape(total * count, K).astype(jnp.bfloat16)


def local(particles, assign, rot_index, group, ctf_table):
    dom_rank = lax.axis_index("dom")
    rot_count = lax.axis_size("rot")
    rot_rank = lax.axis_index("rot")
    dom_count = lax.axis_size("dom")
    classes = CLS_DEV * dom_count
    block = classes // rot_count
    owners_per_block = block // CLS_DEV
    total = 8 * rot_count
    count = particles.shape[0]

    ctf_rows = ctf_table[group]
    ctf_cols = jnp.repeat(ctf_rows, MFREQ, axis=1)
    spec = particles.astype(jnp.float32)
    half = K // 2
    weighted = derotate(spec[:, :half], spec[:, half:], rot_index, ctf_cols, total)
    first_class = rot_rank * block
    member = (
        (first_class + jnp.arange(block, dtype=jnp.int32))[:, None] == assign[None, :]
    ).astype(jnp.float32)
    numer = jnp.dot(
        member, weighted, precision=lax.Precision.HIGHEST, preferred_element_type=jnp.float32
    )
    denom = jnp.dot(
        member,
        ctf_rows * ctf_rows,
        precision=lax.Precision.HIGHEST,
        preferred_element_type=jnp.float32,
    )
    chunks = dom_count
    width = K // chunks
    per_chunk = width // MFREQ
    payload = jnp.concatenate(
        [
            numer.reshape(block, chunks, width).transpose(1, 0, 2),
            jnp.broadcast_to(denom[None], (chunks, block, CYCLES)),
        ],
        axis=2,
    )
    summed = jnp.sum(lax.all_to_all(payload, "dom", 0, 0, tiled=True), axis=0)
    numer_chunk = summed[:, :width].reshape(block, per_chunk, MFREQ)
    first_cycle = (dom_rank * per_chunk) % CYCLES
    denom_chunk = lax.dynamic_slice_in_dim(summed[:, width:], first_cycle, per_chunk, 1)
    plain_chunk = (numer_chunk / (denom_chunk[:, :, None] + 1.0)).reshape(block, width)
    plain = lax.all_to_all(
        jnp.broadcast_to(plain_chunk[None], (chunks, block, width)), "dom", 0, 0, tiled=True
    )
    plain = plain.transpose(1, 0, 2).reshape(block, K)
    spread = jnp.mean(plain * plain, axis=1)
    refs_f32 = plain / jnp.sqrt(spread + 1e-06)[:, None]
    refs_block = refs_f32.astype(jnp.bfloat16)

    others = rot_count - 1
    pairs = []
    for plane in range(rot_count):
        for sender in range(owners_per_block * others):
            owner = plane * owners_per_block + sender // others
            target = (plane + 1 + sender % others) % rot_count
            pairs.append((sender * rot_count + plane, owner * rot_count + target))
    sent = lax.dynamic_slice_in_dim(
        refs_block, jnp.minimum(dom_rank // others, owners_per_block - 1) * CLS_DEV, CLS_DEV, 0
    )
    got = lax.ppermute(sent, ("dom", "rot"), pairs)
    mine = lax.dynamic_slice_in_dim(refs_block, (dom_rank % owners_per_block) * CLS_DEV, CLS_DEV, 0)
    refs = jnp.where((dom_rank // owners_per_block) == rot_rank, mine, got)
    modulated = (spec * jnp.concatenate([ctf_cols, ctf_cols], axis=1)).astype(jnp.bfloat16)
    turned = rotate_all(refs_block.astype(jnp.float32), total)
    found = lax.dot_general(
        modulated, turned, (((1,), (1,)), ((), ())), preferred_element_type=jnp.float32
    )
    best = jnp.max(found.reshape(count, total, block), axis=1) * (1.0 / math.sqrt(K))
    best_scores = lax.all_to_all(best, "rot", 0, 1, tiled=True)

    return (refs, best_scores)


def solution(mesh):
    in_specs = (P("dom", None), P("dom"), P("dom"), P("dom"), P())
    out_specs = (P("dom", None), P(("dom", "rot"), None))
    return jax.shard_map(local, mesh=mesh, in_specs=in_specs, out_specs=out_specs, check_vma=False)
```

```python
import math

import jax
import jax.numpy as jnp
from jax import lax
from jax.sharding import PartitionSpec as P

CYCLES = 64
MFREQ = 64
CLS_DEV = 6
K = 8192


def angles(index, total):
    freqs = jnp.arange(MFREQ, dtype=jnp.int32)
    phase = freqs[None, :] * index[:, None] % total
    return phase.astype(jnp.float32) * (2.0 * math.pi / total)


def derotate(real_part, imag_part, rotation, ctf_cols, total):
    angle = angles(rotation, total)
    cosine = jnp.tile(jnp.cos(angle), (1, CYCLES))
    sine = jnp.tile(jnp.sin(angle), (1, CYCLES))
    return jnp.concatenate(
        [
            (real_part * cosine + imag_part * sine) * ctf_cols,
            (imag_part * cosine - real_part * sine) * ctf_cols,
        ],
        axis=1,
    )


def rotate_all(refs, turns, total):
    count = refs.shape[0]
    half = K // 2
    real_part = refs[None, :, :half]
    imag_part = refs[None, :, half:]
    angle = angles(jnp.arange(turns, dtype=jnp.int32), total)
    cosine = jnp.tile(jnp.cos(angle), (1, CYCLES))[:, None, :]
    sine = jnp.tile(jnp.sin(angle), (1, CYCLES))[:, None, :]
    turned = jnp.concatenate(
        [real_part * cosine - imag_part * sine, real_part * sine + imag_part * cosine], axis=2
    )
    return turned.reshape(turns * count, K).astype(jnp.bfloat16)


def local(particles, assign, rot_index, group, ctf_table):
    dom_rank = lax.axis_index("dom")
    rot_count = lax.axis_size("rot")
    rot_rank = lax.axis_index("rot")
    dom_count = lax.axis_size("dom")
    classes = CLS_DEV * dom_count
    block = classes // rot_count
    owners_per_block = block // CLS_DEV
    total = 8 * rot_count
    count = particles.shape[0]

    ctf_rows = ctf_table[group]
    ctf_cols = jnp.repeat(ctf_rows, MFREQ, axis=1)
    spec = particles.astype(jnp.float32)
    half = K // 2
    weighted = derotate(spec[:, :half], spec[:, half:], rot_index, ctf_cols, total)
    first_class = rot_rank * block
    member = (
        (first_class + jnp.arange(block, dtype=jnp.int32))[:, None] == assign[None, :]
    ).astype(jnp.float32)
    numer = jnp.dot(
        member, weighted, precision=lax.Precision.HIGHEST, preferred_element_type=jnp.float32
    )
    denom = jnp.dot(
        member,
        ctf_rows * ctf_rows,
        precision=lax.Precision.HIGHEST,
        preferred_element_type=jnp.float32,
    )
    chunks = dom_count
    width = K // chunks
    per_chunk = width // MFREQ
    payload = jnp.concatenate(
        [
            numer.reshape(block, chunks, width).transpose(1, 0, 2),
            jnp.broadcast_to(denom[None], (chunks, block, CYCLES)),
        ],
        axis=2,
    )
    summed = jnp.sum(lax.all_to_all(payload, "dom", 0, 0, tiled=True), axis=0)
    numer_chunk = summed[:, :width].reshape(block, per_chunk, MFREQ)
    first_cycle = (dom_rank * per_chunk) % CYCLES
    denom_chunk = lax.dynamic_slice_in_dim(summed[:, width:], first_cycle, per_chunk, 1)
    plain_chunk = (numer_chunk / (denom_chunk[:, :, None] + 1.0)).reshape(block, width)
    plain = lax.all_to_all(
        jnp.broadcast_to(plain_chunk[None], (chunks, block, width)), "dom", 0, 0, tiled=True
    )
    plain = plain.transpose(1, 0, 2).reshape(block, K)
    spread = jnp.mean(plain * plain, axis=1)
    refs_f32 = plain / jnp.sqrt(spread + 1e-06)[:, None]
    refs_block = refs_f32.astype(jnp.bfloat16)

    others = rot_count - 1
    pairs = []
    for plane in range(rot_count):
        for sender in range(owners_per_block * others):
            owner = plane * owners_per_block + sender // others
            target = (plane + 1 + sender % others) % rot_count
            pairs.append((sender * rot_count + plane, owner * rot_count + target))
    sent = lax.dynamic_slice_in_dim(
        refs_block, jnp.minimum(dom_rank // others, owners_per_block - 1) * CLS_DEV, CLS_DEV, 0
    )
    got = lax.ppermute(sent, ("dom", "rot"), pairs)
    mine = lax.dynamic_slice_in_dim(refs_block, (dom_rank % owners_per_block) * CLS_DEV, CLS_DEV, 0)
    refs = jnp.where((dom_rank // owners_per_block) == rot_rank, mine, got)
    modulated = (spec * jnp.concatenate([ctf_cols, ctf_cols], axis=1)).astype(jnp.bfloat16)
    quarter = total // 4
    real_part = modulated[:, :half]
    imag_part = modulated[:, half:]
    freq = jnp.arange(half, dtype=jnp.int32) % MFREQ
    variants = []
    for u in range(4):
        step = (freq * u) % 4
        re_u = jnp.where(step == 0, real_part, jnp.where(step == 1, imag_part, jnp.where(step == 2, -real_part, -imag_part)))
        im_u = jnp.where(step == 0, imag_part, jnp.where(step == 1, -real_part, jnp.where(step == 2, -imag_part, real_part)))
        variants.append(jnp.concatenate([re_u, im_u], axis=1))
    stacked = jnp.concatenate(variants, axis=0)
    turned = rotate_all(refs_block.astype(jnp.float32), quarter, total)
    found = lax.dot_general(
        stacked, turned, (((1,), (1,)), ((), ())), preferred_element_type=jnp.float32
    )
    best = jnp.max(found.reshape(4, count, quarter, block), axis=(0, 2)) * (1.0 / math.sqrt(K))
    best_scores = lax.all_to_all(best, "rot", 0, 1, tiled=True)

    return (refs, best_scores)


def solution(mesh):
    in_specs = (P("dom", None), P("dom"), P("dom"), P("dom"), P())
    out_specs = (P("dom", None), P(("dom", "rot"), None))
    return jax.shard_map(local, mesh=mesh, in_specs=in_specs, out_specs=out_specs, check_vma=False)
```

```python
import math

import jax
import jax.numpy as jnp
from jax import lax
from jax.sharding import PartitionSpec as P

CYCLES = 64
MFREQ = 64
CLS_DEV = 6
K = 8192


def column_angles(index, total, width):
    freqs = lax.broadcasted_iota(jnp.int32, (index.shape[0], width), 1) % MFREQ
    phase = freqs * index[:, None] % total
    return phase.astype(jnp.float32) * (2.0 * math.pi / total)


def derotate(real_part, imag_part, rotation, ctf_cols, total):
    angle = column_angles(rotation, total, real_part.shape[1])
    cosine = jnp.cos(angle)
    sine = jnp.sin(angle)
    return jnp.concatenate(
        [
            (real_part * cosine + imag_part * sine) * ctf_cols,
            (imag_part * cosine - real_part * sine) * ctf_cols,
        ],
        axis=1,
    )


def rotate_all(refs, turns, total):
    count = refs.shape[0]
    half = K // 2
    real_part = refs[None, :, :half]
    imag_part = refs[None, :, half:]
    angle = column_angles(jnp.arange(turns, dtype=jnp.int32), total, half)
    cosine = jnp.cos(angle)[:, None, :]
    sine = jnp.sin(angle)[:, None, :]
    turned = jnp.concatenate(
        [real_part * cosine - imag_part * sine, real_part * sine + imag_part * cosine], axis=2
    )
    return turned.reshape(turns * count, K).astype(jnp.bfloat16)


def local(particles, assign, rot_index, group, ctf_table):
    dom_rank = lax.axis_index("dom")
    rot_count = lax.axis_size("rot")
    rot_rank = lax.axis_index("rot")
    dom_count = lax.axis_size("dom")
    classes = CLS_DEV * dom_count
    block = classes // rot_count
    owners_per_block = block // CLS_DEV
    total = 8 * rot_count
    count = particles.shape[0]

    ctf_rows = ctf_table[group]
    ctf_cols = jnp.repeat(ctf_rows, MFREQ, axis=1)
    spec = particles.astype(jnp.float32)
    half = K // 2
    weighted = derotate(spec[:, :half], spec[:, half:], rot_index, ctf_cols, total)
    first_class = rot_rank * block
    member = (
        (first_class + jnp.arange(block, dtype=jnp.int32))[:, None] == assign[None, :]
    ).astype(jnp.float32)
    numer = jnp.dot(
        member, weighted, precision=lax.Precision.HIGHEST, preferred_element_type=jnp.float32
    )
    denom = jnp.dot(
        member,
        ctf_rows * ctf_rows,
        precision=lax.Precision.HIGHEST,
        preferred_element_type=jnp.float32,
    )
    chunks = dom_count
    width = K // chunks
    per_chunk = width // MFREQ
    payload = jnp.concatenate(
        [
            numer.reshape(block, chunks, width).transpose(1, 0, 2),
            jnp.broadcast_to(denom[None], (chunks, block, CYCLES)),
        ],
        axis=2,
    )
    summed = jnp.sum(lax.all_to_all(payload, "dom", 0, 0, tiled=True), axis=0)
    numer_chunk = summed[:, :width].reshape(block, per_chunk, MFREQ)
    first_cycle = (dom_rank * per_chunk) % CYCLES
    denom_chunk = lax.dynamic_slice_in_dim(summed[:, width:], first_cycle, per_chunk, 1)
    plain_chunk = (numer_chunk / (denom_chunk[:, :, None] + 1.0)).reshape(block, width)
    plain = lax.all_to_all(
        jnp.broadcast_to(plain_chunk[None], (chunks, block, width)), "dom", 0, 0, tiled=True
    )
    plain = plain.transpose(1, 0, 2).reshape(block, K)
    spread = jnp.mean(plain * plain, axis=1)
    refs_f32 = plain / jnp.sqrt(spread + 1e-06)[:, None]
    refs_block = refs_f32.astype(jnp.bfloat16)

    others = rot_count - 1
    pairs = []
    for plane in range(rot_count):
        for sender in range(owners_per_block * others):
            owner = plane * owners_per_block + sender // others
            target = (plane + 1 + sender % others) % rot_count
            pairs.append((sender * rot_count + plane, owner * rot_count + target))
    sent = lax.dynamic_slice_in_dim(
        refs_block, jnp.minimum(dom_rank // others, owners_per_block - 1) * CLS_DEV, CLS_DEV, 0
    )
    got = lax.ppermute(sent, ("dom", "rot"), pairs)
    mine = lax.dynamic_slice_in_dim(refs_block, (dom_rank % owners_per_block) * CLS_DEV, CLS_DEV, 0)
    refs = jnp.where((dom_rank // owners_per_block) == rot_rank, mine, got)
    modulated = (spec * jnp.concatenate([ctf_cols, ctf_cols], axis=1)).astype(jnp.bfloat16)
    quarter = total // 4
    real_part = modulated[:, :half]
    imag_part = modulated[:, half:]
    freq = jnp.arange(half, dtype=jnp.int32) % MFREQ
    variants = []
    for u in range(4):
        step = (freq * u) % 4
        re_u = jnp.where(step == 0, real_part, jnp.where(step == 1, imag_part, jnp.where(step == 2, -real_part, -imag_part)))
        im_u = jnp.where(step == 0, imag_part, jnp.where(step == 1, -real_part, jnp.where(step == 2, -imag_part, real_part)))
        variants.append(jnp.concatenate([re_u, im_u], axis=1))
    stacked = jnp.concatenate(variants, axis=0)
    turned = rotate_all(refs_block.astype(jnp.float32), quarter, total)
    found = lax.dot_general(
        stacked, turned, (((1,), (1,)), ((), ())), preferred_element_type=jnp.float32
    )
    best = jnp.max(found.reshape(4, count, quarter, block), axis=(0, 2)) * (1.0 / math.sqrt(K))
    best_scores = lax.all_to_all(best, "rot", 0, 1, tiled=True)

    return (refs, best_scores)


def solution(mesh):
    in_specs = (P("dom", None), P("dom"), P("dom"), P("dom"), P())
    out_specs = (P("dom", None), P(("dom", "rot"), None))
    return jax.shard_map(local, mesh=mesh, in_specs=in_specs, out_specs=out_specs, check_vma=False)
```

```python
import math

import jax
import jax.numpy as jnp
from jax import lax
from jax.experimental import pallas as pl
from jax.sharding import PartitionSpec as P

CYCLES = 64
MFREQ = 64
CLS_DEV = 6
K = 8192


def column_angles(index, total, width):
    freqs = lax.broadcasted_iota(jnp.int32, (index.shape[0], width), 1) % MFREQ
    phase = freqs * index[:, None] % total
    return phase.astype(jnp.float32) * (2.0 * math.pi / total)


def prologue_kernel(x_ref, cos_ref, sin_ref, ctf_ref, w_ref, mod_ref):
    half = x_ref.shape[1] // 2
    lanes = cos_ref.shape[1]
    cosine = cos_ref[...]
    sine = sin_ref[...]
    low = lax.broadcasted_iota(jnp.int32, cosine.shape, 1) < MFREQ
    for j in range(half // lanes):
        gain = jnp.where(low, ctf_ref[:, 2 * j : 2 * j + 1], ctf_ref[:, 2 * j + 1 : 2 * j + 2])
        re_cols = pl.ds(j * lanes, lanes)
        im_cols = pl.ds(half + j * lanes, lanes)
        real_part = x_ref[:, re_cols].astype(jnp.float32)
        imag_part = x_ref[:, im_cols].astype(jnp.float32)
        w_ref[:, re_cols] = (real_part * cosine + imag_part * sine) * gain
        w_ref[:, im_cols] = (imag_part * cosine - real_part * sine) * gain
        mod_ref[:, re_cols] = (real_part * gain).astype(jnp.bfloat16)
        mod_ref[:, im_cols] = (imag_part * gain).astype(jnp.bfloat16)


def derotate_and_modulate(particles, rotation, ctf_rows, total):
    angle = column_angles(rotation, total, 2 * MFREQ)
    count = particles.shape[0]
    return pl.pallas_call(
        prologue_kernel,
        out_shape=(
            jax.ShapeDtypeStruct((count, K), jnp.float32),
            jax.ShapeDtypeStruct((count, K), jnp.bfloat16),
        ),
    )(particles, jnp.cos(angle), jnp.sin(angle), ctf_rows)


def rotate_all(refs, turns, total):
    count = refs.shape[0]
    half = K // 2
    real_part = refs[None, :, :half]
    imag_part = refs[None, :, half:]
    angle = column_angles(jnp.arange(turns, dtype=jnp.int32), total, half)
    cosine = jnp.cos(angle)[:, None, :]
    sine = jnp.sin(angle)[:, None, :]
    turned = jnp.concatenate(
        [real_part * cosine - imag_part * sine, real_part * sine + imag_part * cosine], axis=2
    )
    return turned.reshape(turns * count, K).astype(jnp.bfloat16)


def local(particles, assign, rot_index, group, ctf_table):
    dom_rank = lax.axis_index("dom")
    rot_count = lax.axis_size("rot")
    rot_rank = lax.axis_index("rot")
    dom_count = lax.axis_size("dom")
    classes = CLS_DEV * dom_count
    block = classes // rot_count
    owners_per_block = block // CLS_DEV
    total = 8 * rot_count
    count = particles.shape[0]

    ctf_rows = ctf_table[group]
    half = K // 2
    weighted, modulated = derotate_and_modulate(particles, rot_index, ctf_rows, total)
    first_class = rot_rank * block
    member = (
        (first_class + jnp.arange(block, dtype=jnp.int32))[:, None] == assign[None, :]
    ).astype(jnp.float32)
    numer = jnp.dot(
        member, weighted, precision=lax.Precision.HIGHEST, preferred_element_type=jnp.float32
    )
    denom = jnp.dot(
        member,
        ctf_rows * ctf_rows,
        precision=lax.Precision.HIGHEST,
        preferred_element_type=jnp.float32,
    )
    chunks = dom_count
    width = K // chunks
    per_chunk = width // MFREQ
    payload = jnp.concatenate(
        [
            numer.reshape(block, chunks, width).transpose(1, 0, 2),
            jnp.broadcast_to(denom[None], (chunks, block, CYCLES)),
        ],
        axis=2,
    )
    summed = jnp.sum(lax.all_to_all(payload, "dom", 0, 0, tiled=True), axis=0)
    numer_chunk = summed[:, :width].reshape(block, per_chunk, MFREQ)
    first_cycle = (dom_rank * per_chunk) % CYCLES
    denom_chunk = lax.dynamic_slice_in_dim(summed[:, width:], first_cycle, per_chunk, 1)
    plain_chunk = (numer_chunk / (denom_chunk[:, :, None] + 1.0)).reshape(block, width)
    plain = lax.all_to_all(
        jnp.broadcast_to(plain_chunk[None], (chunks, block, width)), "dom", 0, 0, tiled=True
    )
    plain = plain.transpose(1, 0, 2).reshape(block, K)
    spread = jnp.mean(plain * plain, axis=1)
    refs_f32 = plain / jnp.sqrt(spread + 1e-06)[:, None]
    refs_block = refs_f32.astype(jnp.bfloat16)

    others = rot_count - 1
    pairs = []
    for plane in range(rot_count):
        for sender in range(owners_per_block * others):
            owner = plane * owners_per_block + sender // others
            target = (plane + 1 + sender % others) % rot_count
            pairs.append((sender * rot_count + plane, owner * rot_count + target))
    sent = lax.dynamic_slice_in_dim(
        refs_block, jnp.minimum(dom_rank // others, owners_per_block - 1) * CLS_DEV, CLS_DEV, 0
    )
    got = lax.ppermute(sent, ("dom", "rot"), pairs)
    mine = lax.dynamic_slice_in_dim(refs_block, (dom_rank % owners_per_block) * CLS_DEV, CLS_DEV, 0)
    refs = jnp.where((dom_rank // owners_per_block) == rot_rank, mine, got)
    quarter = total // 4
    real_part = modulated[:, :half]
    imag_part = modulated[:, half:]
    freq = jnp.arange(half, dtype=jnp.int32) % MFREQ
    variants = []
    for u in range(4):
        step = (freq * u) % 4
        re_u = jnp.where(step == 0, real_part, jnp.where(step == 1, imag_part, jnp.where(step == 2, -real_part, -imag_part)))
        im_u = jnp.where(step == 0, imag_part, jnp.where(step == 1, -real_part, jnp.where(step == 2, -imag_part, real_part)))
        variants.append(jnp.concatenate([re_u, im_u], axis=1))
    stacked = jnp.concatenate(variants, axis=0)
    turned = rotate_all(refs_block.astype(jnp.float32), quarter, total)
    found = lax.dot_general(
        stacked, turned, (((1,), (1,)), ((), ())), preferred_element_type=jnp.float32
    )
    best = jnp.max(found.reshape(4, count, quarter, block), axis=(0, 2)) * (1.0 / math.sqrt(K))
    best_scores = lax.all_to_all(best, "rot", 0, 1, tiled=True)

    return (refs, best_scores)


def solution(mesh):
    in_specs = (P("dom", None), P("dom"), P("dom"), P("dom"), P())
    out_specs = (P("dom", None), P(("dom", "rot"), None))
    return jax.shard_map(local, mesh=mesh, in_specs=in_specs, out_specs=out_specs, check_vma=False)
```

```python
import math

import jax
import jax.numpy as jnp
from jax import lax
from jax.experimental import pallas as pl
from jax.sharding import PartitionSpec as P

CYCLES = 64
MFREQ = 64
CLS_DEV = 6
K = 8192


def column_angles(index, total, width):
    freqs = lax.broadcasted_iota(jnp.int32, (index.shape[0], width), 1) % MFREQ
    phase = freqs * index[:, None] % total
    return phase.astype(jnp.float32) * (2.0 * math.pi / total)


def prologue_kernel(x_ref, cos_ref, sin_ref, ctf_ref, w_ref, mod_ref):
    half = x_ref.shape[1] // 2
    lanes = cos_ref.shape[1]
    cosine = cos_ref[...]
    sine = sin_ref[...]
    low = lax.broadcasted_iota(jnp.int32, cosine.shape, 1) < MFREQ
    for j in range(half // lanes):
        gain = jnp.where(low, ctf_ref[:, 2 * j : 2 * j + 1], ctf_ref[:, 2 * j + 1 : 2 * j + 2])
        re_cols = pl.ds(j * lanes, lanes)
        im_cols = pl.ds(half + j * lanes, lanes)
        real_part = x_ref[:, re_cols].astype(jnp.float32)
        imag_part = x_ref[:, im_cols].astype(jnp.float32)
        w_ref[:, re_cols] = (real_part * cosine + imag_part * sine) * gain
        w_ref[:, im_cols] = (imag_part * cosine - real_part * sine) * gain
        mod_ref[:, re_cols] = (real_part * gain).astype(jnp.bfloat16)
        mod_ref[:, im_cols] = (imag_part * gain).astype(jnp.bfloat16)


def derotate_and_modulate(particles, rotation, ctf_rows, total):
    angle = column_angles(rotation, total, 2 * MFREQ)
    count = particles.shape[0]
    return pl.pallas_call(
        prologue_kernel,
        out_shape=(
            jax.ShapeDtypeStruct((count, K), jnp.float32),
            jax.ShapeDtypeStruct((count, K), jnp.bfloat16),
        ),
    )(particles, jnp.cos(angle), jnp.sin(angle), ctf_rows)


def rotate_all(refs, turns, total):
    count = refs.shape[0]
    half = K // 2
    real_part = refs[None, :, :half]
    imag_part = refs[None, :, half:]
    angle = column_angles(jnp.arange(turns, dtype=jnp.int32), total, half)
    cosine = jnp.cos(angle)[:, None, :]
    sine = jnp.sin(angle)[:, None, :]
    turned = jnp.concatenate(
        [real_part * cosine - imag_part * sine, real_part * sine + imag_part * cosine], axis=2
    )
    return turned.reshape(turns * count, K).astype(jnp.bfloat16)


def local(particles, assign, rot_index, group, ctf_table):
    dom_rank = lax.axis_index("dom")
    rot_count = lax.axis_size("rot")
    rot_rank = lax.axis_index("rot")
    dom_count = lax.axis_size("dom")
    classes = CLS_DEV * dom_count
    block = classes // rot_count
    owners_per_block = block // CLS_DEV
    total = 8 * rot_count
    count = particles.shape[0]

    ctf_rows = ctf_table[group]
    half = K // 2
    weighted, modulated = derotate_and_modulate(particles, rot_index, ctf_rows, total)
    first_class = rot_rank * block
    member = (
        (first_class + jnp.arange(block, dtype=jnp.int32))[:, None] == assign[None, :]
    ).astype(jnp.float32)
    numer = jnp.dot(
        member, weighted, precision=lax.Precision.HIGHEST, preferred_element_type=jnp.float32
    )
    denom = jnp.dot(
        member,
        ctf_rows * ctf_rows,
        precision=lax.Precision.HIGHEST,
        preferred_element_type=jnp.float32,
    )
    chunks = dom_count
    width = K // chunks
    per_chunk = width // MFREQ
    payload = jnp.concatenate(
        [
            numer.reshape(block, chunks, width).transpose(1, 0, 2).reshape(chunks, block * width),
            jnp.broadcast_to(denom.reshape(1, block * CYCLES), (chunks, block * CYCLES)),
        ],
        axis=1,
    )
    summed = jnp.sum(lax.all_to_all(payload, "dom", 0, 0, tiled=True), axis=0)
    numer_chunk = summed[: block * width].reshape(block, per_chunk, MFREQ)
    denom_all = summed[block * width :].reshape(block, CYCLES)
    first_cycle = (dom_rank * per_chunk) % CYCLES
    denom_chunk = lax.dynamic_slice_in_dim(denom_all, first_cycle, per_chunk, 1)
    plain_chunk = (numer_chunk / (denom_chunk[:, :, None] + 1.0)).reshape(block, width)
    plain = lax.all_to_all(
        jnp.broadcast_to(plain_chunk[None], (chunks, block, width)), "dom", 0, 0, tiled=True
    )
    plain = plain.transpose(1, 0, 2).reshape(block, K)
    spread = jnp.mean(plain * plain, axis=1)
    refs_f32 = plain / jnp.sqrt(spread + 1e-06)[:, None]
    refs_block = refs_f32.astype(jnp.bfloat16)

    others = rot_count - 1
    pairs = []
    for plane in range(rot_count):
        for sender in range(owners_per_block * others):
            owner = plane * owners_per_block + sender // others
            target = (plane + 1 + sender % others) % rot_count
            pairs.append((sender * rot_count + plane, owner * rot_count + target))
    sent = lax.dynamic_slice_in_dim(
        refs_block, jnp.minimum(dom_rank // others, owners_per_block - 1) * CLS_DEV, CLS_DEV, 0
    )
    got = lax.ppermute(sent, ("dom", "rot"), pairs)
    mine = lax.dynamic_slice_in_dim(refs_block, (dom_rank % owners_per_block) * CLS_DEV, CLS_DEV, 0)
    refs = jnp.where((dom_rank // owners_per_block) == rot_rank, mine, got)
    quarter = total // 4
    real_part = modulated[:, :half]
    imag_part = modulated[:, half:]
    freq = jnp.arange(half, dtype=jnp.int32) % MFREQ
    variants = []
    for u in range(4):
        step = (freq * u) % 4
        re_u = jnp.where(step == 0, real_part, jnp.where(step == 1, imag_part, jnp.where(step == 2, -real_part, -imag_part)))
        im_u = jnp.where(step == 0, imag_part, jnp.where(step == 1, -real_part, jnp.where(step == 2, -imag_part, real_part)))
        variants.append(jnp.concatenate([re_u, im_u], axis=1))
    stacked = jnp.concatenate(variants, axis=0)
    turned = rotate_all(refs_block.astype(jnp.float32), quarter, total)
    found = lax.dot_general(
        stacked, turned, (((1,), (1,)), ((), ())), preferred_element_type=jnp.float32
    )
    best = jnp.max(found.reshape(4, count, quarter, block), axis=(0, 2)) * (1.0 / math.sqrt(K))
    best_scores = lax.all_to_all(best, "rot", 0, 1, tiled=True)

    return (refs, best_scores)


def solution(mesh):
    in_specs = (P("dom", None), P("dom"), P("dom"), P("dom"), P())
    out_specs = (P("dom", None), P(("dom", "rot"), None))
    return jax.shard_map(local, mesh=mesh, in_specs=in_specs, out_specs=out_specs, check_vma=False)
```

```python
import math

import jax
import jax.numpy as jnp
from jax import lax
from jax.experimental import pallas as pl
from jax.experimental.pallas import tpu as pltpu
from jax.sharding import PartitionSpec as P

CYCLES = 64
MFREQ = 64
CLS_DEV = 6
K = 8192


def column_angles(index, total, width):
    freqs = lax.broadcasted_iota(jnp.int32, (index.shape[0], width), 1) % MFREQ
    phase = freqs * index[:, None] % total
    return phase.astype(jnp.float32) * (2.0 * math.pi / total)


def split_dot(member, value):
    high = value.astype(jnp.bfloat16)
    rest = value - high.astype(jnp.float32)
    mid = rest.astype(jnp.bfloat16)
    low = (rest - mid.astype(jnp.float32)).astype(jnp.bfloat16)
    total = jnp.dot(member, high, preferred_element_type=jnp.float32)
    total = total + jnp.dot(member, mid, preferred_element_type=jnp.float32)
    return total + jnp.dot(member, low, preferred_element_type=jnp.float32)


def prologue_kernel(x_ref, cos_ref, sin_ref, ctf_ref, member_ref, pay_ref, mod_ref, w_ref):
    half = x_ref.shape[1] // 2
    lanes = cos_ref.shape[1]
    chunks, _, width = pay_ref.shape
    width -= ctf_ref.shape[1]
    cosine = cos_ref[...]
    sine = sin_ref[...]
    low = lax.broadcasted_iota(jnp.int32, cosine.shape, 1) < MFREQ
    for j in range(half // lanes):
        gain = jnp.where(low, ctf_ref[:, 2 * j : 2 * j + 1], ctf_ref[:, 2 * j + 1 : 2 * j + 2])
        re_cols = pl.ds(j * lanes, lanes)
        im_cols = pl.ds(half + j * lanes, lanes)
        real_part = x_ref[:, re_cols].astype(jnp.float32)
        imag_part = x_ref[:, im_cols].astype(jnp.float32)
        w_ref[:, re_cols] = (real_part * cosine + imag_part * sine) * gain
        w_ref[:, im_cols] = (imag_part * cosine - real_part * sine) * gain
        mod_ref[:, re_cols] = (real_part * gain).astype(jnp.bfloat16)
        mod_ref[:, im_cols] = (imag_part * gain).astype(jnp.bfloat16)
    member = member_ref[...]
    gains = ctf_ref[...]
    denom = split_dot(member, gains * gains)
    numer = split_dot(member, w_ref[...])
    for x in range(chunks):
        pay_ref[x, :, :width] = numer[:, x * width : (x + 1) * width]
        pay_ref[x, :, width:] = denom


def derotate_and_sum(particles, rotation, ctf_rows, member, chunks, total):
    angle = column_angles(rotation, total, 2 * MFREQ)
    count = particles.shape[0]
    block = member.shape[0]
    return pl.pallas_call(
        prologue_kernel,
        out_shape=(
            jax.ShapeDtypeStruct((chunks, block, K // chunks + CYCLES), jnp.float32),
            jax.ShapeDtypeStruct((count, K), jnp.bfloat16),
        ),
        scratch_shapes=[pltpu.VMEM((count, K), jnp.float32)],
    )(particles, jnp.cos(angle), jnp.sin(angle), ctf_rows, member)


def rotate_all(refs, turns, total):
    count = refs.shape[0]
    half = K // 2
    real_part = refs[None, :, :half]
    imag_part = refs[None, :, half:]
    angle = column_angles(jnp.arange(turns, dtype=jnp.int32), total, half)
    cosine = jnp.cos(angle)[:, None, :]
    sine = jnp.sin(angle)[:, None, :]
    turned = jnp.concatenate(
        [real_part * cosine - imag_part * sine, real_part * sine + imag_part * cosine], axis=2
    )
    return turned.reshape(turns * count, K).astype(jnp.bfloat16)


def local(particles, assign, rot_index, group, ctf_table):
    dom_rank = lax.axis_index("dom")
    rot_count = lax.axis_size("rot")
    rot_rank = lax.axis_index("rot")
    dom_count = lax.axis_size("dom")
    classes = CLS_DEV * dom_count
    block = classes // rot_count
    owners_per_block = block // CLS_DEV
    total = 8 * rot_count
    count = particles.shape[0]

    ctf_rows = ctf_table[group]
    half = K // 2
    first_class = rot_rank * block
    member = (
        (first_class + jnp.arange(block, dtype=jnp.int32))[:, None] == assign[None, :]
    ).astype(jnp.bfloat16)
    chunks = dom_count
    width = K // chunks
    per_chunk = width // MFREQ
    payload, modulated = derotate_and_sum(particles, rot_index, ctf_rows, member, chunks, total)
    summed = jnp.sum(lax.all_to_all(payload, "dom", 0, 0, tiled=True), axis=0)
    numer_chunk = summed[:, :width].reshape(block, per_chunk, MFREQ)
    first_cycle = (dom_rank * per_chunk) % CYCLES
    denom_chunk = lax.dynamic_slice_in_dim(summed[:, width:], first_cycle, per_chunk, 1)
    plain_chunk = (numer_chunk / (denom_chunk[:, :, None] + 1.0)).reshape(block, width)
    plain = lax.all_to_all(
        jnp.broadcast_to(plain_chunk[None], (chunks, block, width)), "dom", 0, 0, tiled=True
    )
    plain = plain.transpose(1, 0, 2).reshape(block, K)
    spread = jnp.mean(plain * plain, axis=1)
    refs_f32 = plain / jnp.sqrt(spread + 1e-06)[:, None]
    refs_block = refs_f32.astype(jnp.bfloat16)

    others = rot_count - 1
    pairs = []
    for plane in range(rot_count):
        for sender in range(owners_per_block * others):
            owner = plane * owners_per_block + sender // others
            target = (plane + 1 + sender % others) % rot_count
            pairs.append((sender * rot_count + plane, owner * rot_count + target))
    sent = lax.dynamic_slice_in_dim(
        refs_block, jnp.minimum(dom_rank // others, owners_per_block - 1) * CLS_DEV, CLS_DEV, 0
    )
    got = lax.ppermute(sent, ("dom", "rot"), pairs)
    mine = lax.dynamic_slice_in_dim(refs_block, (dom_rank % owners_per_block) * CLS_DEV, CLS_DEV, 0)
    refs = jnp.where((dom_rank // owners_per_block) == rot_rank, mine, got)
    quarter = total // 4
    real_part = modulated[:, :half]
    imag_part = modulated[:, half:]
    freq = jnp.arange(half, dtype=jnp.int32) % MFREQ
    variants = []
    for u in range(4):
        step = (freq * u) % 4
        re_u = jnp.where(step == 0, real_part, jnp.where(step == 1, imag_part, jnp.where(step == 2, -real_part, -imag_part)))
        im_u = jnp.where(step == 0, imag_part, jnp.where(step == 1, -real_part, jnp.where(step == 2, -imag_part, real_part)))
        variants.append(jnp.concatenate([re_u, im_u], axis=1))
    stacked = jnp.concatenate(variants, axis=0)
    turned = rotate_all(refs_block.astype(jnp.float32), quarter, total)
    found = lax.dot_general(
        stacked, turned, (((1,), (1,)), ((), ())), preferred_element_type=jnp.float32
    )
    best = jnp.max(found.reshape(4, count, quarter, block), axis=(0, 2)) * (1.0 / math.sqrt(K))
    best_scores = lax.all_to_all(best, "rot", 0, 1, tiled=True)

    return (refs, best_scores)


def solution(mesh):
    in_specs = (P("dom", None), P("dom"), P("dom"), P("dom"), P())
    out_specs = (P("dom", None), P(("dom", "rot"), None))
    return jax.shard_map(local, mesh=mesh, in_specs=in_specs, out_specs=out_specs, check_vma=False)
```

```python
import math

import jax
import jax.numpy as jnp
from jax import lax
from jax.experimental import pallas as pl
from jax.experimental.pallas import tpu as pltpu
from jax.sharding import PartitionSpec as P

CYCLES = 64
MFREQ = 64
CLS_DEV = 6
K = 8192


def column_angles(index, total, width):
    freqs = lax.broadcasted_iota(jnp.int32, (index.shape[0], width), 1) % MFREQ
    phase = freqs * index[:, None] % total
    return phase.astype(jnp.float32) * (2.0 * math.pi / total)


def split_dot(member, value):
    high = value.astype(jnp.bfloat16)
    rest = value - high.astype(jnp.float32)
    mid = rest.astype(jnp.bfloat16)
    low = (rest - mid.astype(jnp.float32)).astype(jnp.bfloat16)
    total = jnp.dot(member, high, preferred_element_type=jnp.float32)
    total = total + jnp.dot(member, mid, preferred_element_type=jnp.float32)
    return total + jnp.dot(member, low, preferred_element_type=jnp.float32)


def prologue_kernel(
    x_ref, cos_ref, sin_ref, group_ref, table_ref, assign_ref, pay_ref, mod_ref, w_ref, ctf_ref
):
    groups = table_ref.shape[0]
    count = x_ref.shape[0]
    block = pay_ref.shape[1]
    onehot = group_ref[...] == lax.broadcasted_iota(jnp.int32, (count, groups), 1)
    ctf_ref[...] = split_dot(onehot.astype(jnp.bfloat16), table_ref[...])
    first_class = lax.axis_index("rot") * block
    classes = first_class + lax.broadcasted_iota(jnp.int32, (block, count), 0)
    member = (classes == assign_ref[...]).astype(jnp.bfloat16)
    half = x_ref.shape[1] // 2
    lanes = cos_ref.shape[1]
    chunks, _, width = pay_ref.shape
    width -= ctf_ref.shape[1]
    cosine = cos_ref[...]
    sine = sin_ref[...]
    low = lax.broadcasted_iota(jnp.int32, cosine.shape, 1) < MFREQ
    for j in range(half // lanes):
        gain = jnp.where(low, ctf_ref[:, 2 * j : 2 * j + 1], ctf_ref[:, 2 * j + 1 : 2 * j + 2])
        re_cols = pl.ds(j * lanes, lanes)
        im_cols = pl.ds(half + j * lanes, lanes)
        real_part = x_ref[:, re_cols].astype(jnp.float32)
        imag_part = x_ref[:, im_cols].astype(jnp.float32)
        w_ref[:, re_cols] = (real_part * cosine + imag_part * sine) * gain
        w_ref[:, im_cols] = (imag_part * cosine - real_part * sine) * gain
        mod_ref[:, re_cols] = (real_part * gain).astype(jnp.bfloat16)
        mod_ref[:, im_cols] = (imag_part * gain).astype(jnp.bfloat16)
    gains = ctf_ref[...]
    denom = split_dot(member, gains * gains)
    numer = split_dot(member, w_ref[...])
    for x in range(chunks):
        pay_ref[x, :, :width] = numer[:, x * width : (x + 1) * width]
        pay_ref[x, :, width:] = denom


def derotate_and_sum(particles, rotation, group, ctf_table, assign, block, chunks, total):
    angle = column_angles(rotation, total, 2 * MFREQ)
    count = particles.shape[0]
    return pl.pallas_call(
        prologue_kernel,
        out_shape=(
            jax.ShapeDtypeStruct((chunks, block, K // chunks + CYCLES), jnp.float32),
            jax.ShapeDtypeStruct((count, K), jnp.bfloat16),
        ),
        scratch_shapes=[
            pltpu.VMEM((count, K), jnp.float32),
            pltpu.VMEM((count, ctf_table.shape[1]), jnp.float32),
        ],
    )(
        particles,
        jnp.cos(angle),
        jnp.sin(angle),
        group.reshape(count, 1),
        ctf_table,
        assign.reshape(1, count),
    )


def rotate_all(refs, turns, total):
    count = refs.shape[0]
    half = K // 2
    real_part = refs[None, :, :half]
    imag_part = refs[None, :, half:]
    angle = column_angles(jnp.arange(turns, dtype=jnp.int32), total, half)
    cosine = jnp.cos(angle)[:, None, :]
    sine = jnp.sin(angle)[:, None, :]
    turned = jnp.concatenate(
        [real_part * cosine - imag_part * sine, real_part * sine + imag_part * cosine], axis=2
    )
    return turned.reshape(turns * count, K).astype(jnp.bfloat16)


def local(particles, assign, rot_index, group, ctf_table):
    dom_rank = lax.axis_index("dom")
    rot_count = lax.axis_size("rot")
    rot_rank = lax.axis_index("rot")
    dom_count = lax.axis_size("dom")
    classes = CLS_DEV * dom_count
    block = classes // rot_count
    owners_per_block = block // CLS_DEV
    total = 8 * rot_count
    count = particles.shape[0]

    half = K // 2
    chunks = dom_count
    width = K // chunks
    per_chunk = width // MFREQ
    payload, modulated = derotate_and_sum(
        particles, rot_index, group, ctf_table, assign, block, chunks, total
    )
    summed = jnp.sum(lax.all_to_all(payload, "dom", 0, 0, tiled=True), axis=0)
    numer_chunk = summed[:, :width].reshape(block, per_chunk, MFREQ)
    first_cycle = (dom_rank * per_chunk) % CYCLES
    denom_chunk = lax.dynamic_slice_in_dim(summed[:, width:], first_cycle, per_chunk, 1)
    plain_chunk = (numer_chunk / (denom_chunk[:, :, None] + 1.0)).reshape(block, width)
    plain = lax.all_to_all(
        jnp.broadcast_to(plain_chunk[None], (chunks, block, width)), "dom", 0, 0, tiled=True
    )
    plain = plain.transpose(1, 0, 2).reshape(block, K)
    spread = jnp.mean(plain * plain, axis=1)
    refs_f32 = plain / jnp.sqrt(spread + 1e-06)[:, None]
    refs_block = refs_f32.astype(jnp.bfloat16)

    others = rot_count - 1
    pairs = []
    for plane in range(rot_count):
        for sender in range(owners_per_block * others):
            owner = plane * owners_per_block + sender // others
            target = (plane + 1 + sender % others) % rot_count
            pairs.append((sender * rot_count + plane, owner * rot_count + target))
    sent = lax.dynamic_slice_in_dim(
        refs_block, jnp.minimum(dom_rank // others, owners_per_block - 1) * CLS_DEV, CLS_DEV, 0
    )
    got = lax.ppermute(sent, ("dom", "rot"), pairs)
    mine = lax.dynamic_slice_in_dim(refs_block, (dom_rank % owners_per_block) * CLS_DEV, CLS_DEV, 0)
    refs = jnp.where((dom_rank // owners_per_block) == rot_rank, mine, got)
    quarter = total // 4
    real_part = modulated[:, :half]
    imag_part = modulated[:, half:]
    freq = jnp.arange(half, dtype=jnp.int32) % MFREQ
    variants = []
    for u in range(4):
        step = (freq * u) % 4
        re_u = jnp.where(step == 0, real_part, jnp.where(step == 1, imag_part, jnp.where(step == 2, -real_part, -imag_part)))
        im_u = jnp.where(step == 0, imag_part, jnp.where(step == 1, -real_part, jnp.where(step == 2, -imag_part, real_part)))
        variants.append(jnp.concatenate([re_u, im_u], axis=1))
    stacked = jnp.concatenate(variants, axis=0)
    turned = rotate_all(refs_block.astype(jnp.float32), quarter, total)
    found = lax.dot_general(
        stacked, turned, (((1,), (1,)), ((), ())), preferred_element_type=jnp.float32
    )
    best = jnp.max(found.reshape(4, count, quarter, block), axis=(0, 2)) * (1.0 / math.sqrt(K))
    best_scores = lax.all_to_all(best, "rot", 0, 1, tiled=True)

    return (refs, best_scores)


def solution(mesh):
    in_specs = (P("dom", None), P("dom"), P("dom"), P("dom"), P())
    out_specs = (P("dom", None), P(("dom", "rot"), None))
    return jax.shard_map(local, mesh=mesh, in_specs=in_specs, out_specs=out_specs, check_vma=False)
```

```python
import math

import jax
import jax.numpy as jnp
from jax import lax
from jax.experimental import pallas as pl
from jax.experimental.pallas import tpu as pltpu
from jax.sharding import PartitionSpec as P

CYCLES = 64
MFREQ = 64
CLS_DEV = 6
K = 8192


def column_angles(index, total, width):
    freqs = lax.broadcasted_iota(jnp.int32, (index.shape[0], width), 1) % MFREQ
    phase = freqs * index[:, None] % total
    return phase.astype(jnp.float32) * (2.0 * math.pi / total)


def split_dot(member, value):
    high = value.astype(jnp.bfloat16)
    rest = value - high.astype(jnp.float32)
    mid = rest.astype(jnp.bfloat16)
    low = (rest - mid.astype(jnp.float32)).astype(jnp.bfloat16)
    total = jnp.dot(member, high, preferred_element_type=jnp.float32)
    total = total + jnp.dot(member, mid, preferred_element_type=jnp.float32)
    return total + jnp.dot(member, low, preferred_element_type=jnp.float32)


def prologue_kernel(
    x_ref, cos_ref, sin_ref, group_ref, table_ref, assign_ref, pay_ref, mod_ref, w_ref, ctf_ref
):
    count = x_ref.shape[0]
    block = pay_ref.shape[1]
    for p in range(count):
        ctf_ref[pl.ds(p, 1), :] = table_ref[pl.ds(group_ref[p], 1), :]
    first_class = lax.axis_index("rot") * block
    classes = first_class + lax.broadcasted_iota(jnp.int32, (block, count), 0)
    member = (classes == assign_ref[...]).astype(jnp.bfloat16)
    half = x_ref.shape[1] // 2
    lanes = cos_ref.shape[1]
    chunks, _, width = pay_ref.shape
    width -= ctf_ref.shape[1]
    cosine = cos_ref[...]
    sine = sin_ref[...]
    low = lax.broadcasted_iota(jnp.int32, cosine.shape, 1) < MFREQ
    for j in range(half // lanes):
        gain = jnp.where(low, ctf_ref[:, 2 * j : 2 * j + 1], ctf_ref[:, 2 * j + 1 : 2 * j + 2])
        re_cols = pl.ds(j * lanes, lanes)
        im_cols = pl.ds(half + j * lanes, lanes)
        real_part = x_ref[:, re_cols].astype(jnp.float32)
        imag_part = x_ref[:, im_cols].astype(jnp.float32)
        w_ref[:, re_cols] = (real_part * cosine + imag_part * sine) * gain
        w_ref[:, im_cols] = (imag_part * cosine - real_part * sine) * gain
        mod_ref[:, re_cols] = (real_part * gain).astype(jnp.bfloat16)
        mod_ref[:, im_cols] = (imag_part * gain).astype(jnp.bfloat16)
    gains = ctf_ref[...]
    denom = split_dot(member, gains * gains)
    numer = split_dot(member, w_ref[...])
    for x in range(chunks):
        pay_ref[x, :, :width] = numer[:, x * width : (x + 1) * width]
        pay_ref[x, :, width:] = denom


def derotate_and_sum(particles, rotation, group, ctf_table, assign, block, chunks, total):
    angle = column_angles(rotation, total, 2 * MFREQ)
    count = particles.shape[0]
    vmem = pl.BlockSpec(memory_space=pltpu.VMEM)
    return pl.pallas_call(
        prologue_kernel,
        out_shape=(
            jax.ShapeDtypeStruct((chunks, block, K // chunks + CYCLES), jnp.float32),
            jax.ShapeDtypeStruct((count, K), jnp.bfloat16),
        ),
        in_specs=[vmem, vmem, vmem, pl.BlockSpec(memory_space=pltpu.SMEM), vmem, vmem],
        scratch_shapes=[
            pltpu.VMEM((count, K), jnp.float32),
            pltpu.VMEM((count, ctf_table.shape[1]), jnp.float32),
        ],
    )(
        particles,
        jnp.cos(angle),
        jnp.sin(angle),
        group,
        ctf_table,
        assign.reshape(1, count),
    )


def rotate_all(refs, turns, total):
    count = refs.shape[0]
    half = K // 2
    real_part = refs[None, :, :half]
    imag_part = refs[None, :, half:]
    angle = column_angles(jnp.arange(turns, dtype=jnp.int32), total, half)
    cosine = jnp.cos(angle)[:, None, :]
    sine = jnp.sin(angle)[:, None, :]
    turned = jnp.concatenate(
        [real_part * cosine - imag_part * sine, real_part * sine + imag_part * cosine], axis=2
    )
    return turned.reshape(turns * count, K).astype(jnp.bfloat16)


def local(particles, assign, rot_index, group, ctf_table):
    dom_rank = lax.axis_index("dom")
    rot_count = lax.axis_size("rot")
    rot_rank = lax.axis_index("rot")
    dom_count = lax.axis_size("dom")
    classes = CLS_DEV * dom_count
    block = classes // rot_count
    owners_per_block = block // CLS_DEV
    total = 8 * rot_count
    count = particles.shape[0]

    half = K // 2
    chunks = dom_count
    width = K // chunks
    per_chunk = width // MFREQ
    payload, modulated = derotate_and_sum(
        particles, rot_index, group, ctf_table, assign, block, chunks, total
    )
    summed = jnp.sum(lax.all_to_all(payload, "dom", 0, 0, tiled=True), axis=0)
    numer_chunk = summed[:, :width].reshape(block, per_chunk, MFREQ)
    first_cycle = (dom_rank * per_chunk) % CYCLES
    denom_chunk = lax.dynamic_slice_in_dim(summed[:, width:], first_cycle, per_chunk, 1)
    plain_chunk = (numer_chunk / (denom_chunk[:, :, None] + 1.0)).reshape(block, width)
    plain = lax.all_to_all(
        jnp.broadcast_to(plain_chunk[None], (chunks, block, width)), "dom", 0, 0, tiled=True
    )
    plain = plain.transpose(1, 0, 2).reshape(block, K)
    spread = jnp.mean(plain * plain, axis=1)
    refs_f32 = plain / jnp.sqrt(spread + 1e-06)[:, None]
    refs_block = refs_f32.astype(jnp.bfloat16)

    others = rot_count - 1
    pairs = []
    for plane in range(rot_count):
        for sender in range(owners_per_block * others):
            owner = plane * owners_per_block + sender // others
            target = (plane + 1 + sender % others) % rot_count
            pairs.append((sender * rot_count + plane, owner * rot_count + target))
    sent = lax.dynamic_slice_in_dim(
        refs_block, jnp.minimum(dom_rank // others, owners_per_block - 1) * CLS_DEV, CLS_DEV, 0
    )
    got = lax.ppermute(sent, ("dom", "rot"), pairs)
    mine = lax.dynamic_slice_in_dim(refs_block, (dom_rank % owners_per_block) * CLS_DEV, CLS_DEV, 0)
    refs = jnp.where((dom_rank // owners_per_block) == rot_rank, mine, got)
    quarter = total // 4
    real_part = modulated[:, :half]
    imag_part = modulated[:, half:]
    freq = jnp.arange(half, dtype=jnp.int32) % MFREQ
    variants = []
    for u in range(4):
        step = (freq * u) % 4
        re_u = jnp.where(step == 0, real_part, jnp.where(step == 1, imag_part, jnp.where(step == 2, -real_part, -imag_part)))
        im_u = jnp.where(step == 0, imag_part, jnp.where(step == 1, -real_part, jnp.where(step == 2, -imag_part, real_part)))
        variants.append(jnp.concatenate([re_u, im_u], axis=1))
    stacked = jnp.concatenate(variants, axis=0)
    turned = rotate_all(refs_block.astype(jnp.float32), quarter, total)
    found = lax.dot_general(
        stacked, turned, (((1,), (1,)), ((), ())), preferred_element_type=jnp.float32
    )
    best = jnp.max(found.reshape(4, count, quarter, block), axis=(0, 2)) * (1.0 / math.sqrt(K))
    best_scores = lax.all_to_all(best, "rot", 0, 1, tiled=True)

    return (refs, best_scores)


def solution(mesh):
    in_specs = (P("dom", None), P("dom"), P("dom"), P("dom"), P())
    out_specs = (P("dom", None), P(("dom", "rot"), None))
    return jax.shard_map(local, mesh=mesh, in_specs=in_specs, out_specs=out_specs, check_vma=False)
```

```python
import math

import jax
import numpy as np
import jax.numpy as jnp
from jax import lax
from jax.experimental import pallas as pl
from jax.experimental.pallas import tpu as pltpu
from jax.sharding import PartitionSpec as P

CYCLES = 64
MFREQ = 64
CLS_DEV = 6
K = 8192


def column_angles(index, total, width):
    freqs = lax.broadcasted_iota(jnp.int32, (index.shape[0], width), 1) % MFREQ
    phase = freqs * index[:, None] % total
    return phase.astype(jnp.float32) * (2.0 * math.pi / total)


def split_dot(member, value):
    high = value.astype(jnp.bfloat16)
    rest = value - high.astype(jnp.float32)
    mid = rest.astype(jnp.bfloat16)
    low = (rest - mid.astype(jnp.float32)).astype(jnp.bfloat16)
    total = jnp.dot(member, high, preferred_element_type=jnp.float32)
    total = total + jnp.dot(member, mid, preferred_element_type=jnp.float32)
    return total + jnp.dot(member, low, preferred_element_type=jnp.float32)


def prologue_kernel(
    x_ref, cos_ref, sin_ref, rot_ref, group_ref, table_ref, assign_ref,
    pay_ref, mod_ref, w_ref, ctf_ref, cos_scr, sin_scr,
):
    count = x_ref.shape[0]
    block = pay_ref.shape[1]
    for p in range(count):
        ctf_ref[pl.ds(p, 1), :] = table_ref[pl.ds(group_ref[p], 1), :]
        cos_scr[pl.ds(p, 1), :] = cos_ref[pl.ds(rot_ref[p], 1), :]
        sin_scr[pl.ds(p, 1), :] = sin_ref[pl.ds(rot_ref[p], 1), :]
    first_class = lax.axis_index("rot") * block
    classes = first_class + lax.broadcasted_iota(jnp.int32, (block, count), 0)
    member = (classes == assign_ref[...]).astype(jnp.bfloat16)
    half = x_ref.shape[1] // 2
    lanes = cos_ref.shape[1]
    chunks, _, width = pay_ref.shape
    width -= ctf_ref.shape[1]
    cosine = cos_scr[...]
    sine = sin_scr[...]
    low = lax.broadcasted_iota(jnp.int32, cosine.shape, 1) < MFREQ
    for j in range(half // lanes):
        gain = jnp.where(low, ctf_ref[:, 2 * j : 2 * j + 1], ctf_ref[:, 2 * j + 1 : 2 * j + 2])
        re_cols = pl.ds(j * lanes, lanes)
        im_cols = pl.ds(half + j * lanes, lanes)
        real_part = x_ref[:, re_cols].astype(jnp.float32)
        imag_part = x_ref[:, im_cols].astype(jnp.float32)
        w_ref[:, re_cols] = (real_part * cosine + imag_part * sine) * gain
        w_ref[:, im_cols] = (imag_part * cosine - real_part * sine) * gain
        mod_ref[:, re_cols] = (real_part * gain).astype(jnp.bfloat16)
        mod_ref[:, im_cols] = (imag_part * gain).astype(jnp.bfloat16)
    gains = ctf_ref[...]
    denom = split_dot(member, gains * gains)
    numer = split_dot(member, w_ref[...])
    for x in range(chunks):
        pay_ref[x, :, :width] = numer[:, x * width : (x + 1) * width]
        pay_ref[x, :, width:] = denom


def derotate_and_sum(particles, rotation, group, ctf_table, assign, block, chunks, total):
    phase = (np.arange(2 * MFREQ)[None, :] % MFREQ) * np.arange(total)[:, None] % total
    angle = phase.astype(np.float32) * np.float32(2.0 * math.pi / total)
    count = particles.shape[0]
    smem = pl.BlockSpec(memory_space=pltpu.SMEM)
    vmem = pl.BlockSpec(memory_space=pltpu.VMEM)
    return pl.pallas_call(
        prologue_kernel,
        out_shape=(
            jax.ShapeDtypeStruct((chunks, block, K // chunks + CYCLES), jnp.float32),
            jax.ShapeDtypeStruct((count, K), jnp.bfloat16),
        ),
        in_specs=[vmem, vmem, vmem, smem, smem, vmem, vmem],
        scratch_shapes=[
            pltpu.VMEM((count, K), jnp.float32),
            pltpu.VMEM((count, ctf_table.shape[1]), jnp.float32),
            pltpu.VMEM((count, 2 * MFREQ), jnp.float32),
            pltpu.VMEM((count, 2 * MFREQ), jnp.float32),
        ],
    )(
        particles,
        jnp.asarray(np.cos(angle)),
        jnp.asarray(np.sin(angle)),
        rotation,
        group,
        ctf_table,
        assign.reshape(1, count),
    )


def rotate_all(refs, turns, total):
    count = refs.shape[0]
    half = K // 2
    real_part = refs[None, :, :half]
    imag_part = refs[None, :, half:]
    angle = column_angles(jnp.arange(turns, dtype=jnp.int32), total, half)
    cosine = jnp.cos(angle)[:, None, :]
    sine = jnp.sin(angle)[:, None, :]
    turned = jnp.concatenate(
        [real_part * cosine - imag_part * sine, real_part * sine + imag_part * cosine], axis=2
    )
    return turned.reshape(turns * count, K).astype(jnp.bfloat16)


def local(particles, assign, rot_index, group, ctf_table):
    dom_rank = lax.axis_index("dom")
    rot_count = lax.axis_size("rot")
    rot_rank = lax.axis_index("rot")
    dom_count = lax.axis_size("dom")
    classes = CLS_DEV * dom_count
    block = classes // rot_count
    owners_per_block = block // CLS_DEV
    total = 8 * rot_count
    count = particles.shape[0]

    half = K // 2
    chunks = dom_count
    width = K // chunks
    per_chunk = width // MFREQ
    payload, modulated = derotate_and_sum(
        particles, rot_index, group, ctf_table, assign, block, chunks, total
    )
    summed = jnp.sum(lax.all_to_all(payload, "dom", 0, 0, tiled=True), axis=0)
    numer_chunk = summed[:, :width].reshape(block, per_chunk, MFREQ)
    first_cycle = (dom_rank * per_chunk) % CYCLES
    denom_chunk = lax.dynamic_slice_in_dim(summed[:, width:], first_cycle, per_chunk, 1)
    plain_chunk = (numer_chunk / (denom_chunk[:, :, None] + 1.0)).reshape(block, width)
    plain = lax.all_to_all(
        jnp.broadcast_to(plain_chunk[None], (chunks, block, width)), "dom", 0, 0, tiled=True
    )
    plain = plain.transpose(1, 0, 2).reshape(block, K)
    spread = jnp.mean(plain * plain, axis=1)
    refs_f32 = plain / jnp.sqrt(spread + 1e-06)[:, None]
    refs_block = refs_f32.astype(jnp.bfloat16)

    others = rot_count - 1
    pairs = []
    for plane in range(rot_count):
        for sender in range(owners_per_block * others):
            owner = plane * owners_per_block + sender // others
            target = (plane + 1 + sender % others) % rot_count
            pairs.append((sender * rot_count + plane, owner * rot_count + target))
    sent = lax.dynamic_slice_in_dim(
        refs_block, jnp.minimum(dom_rank // others, owners_per_block - 1) * CLS_DEV, CLS_DEV, 0
    )
    got = lax.ppermute(sent, ("dom", "rot"), pairs)
    mine = lax.dynamic_slice_in_dim(refs_block, (dom_rank % owners_per_block) * CLS_DEV, CLS_DEV, 0)
    refs = jnp.where((dom_rank // owners_per_block) == rot_rank, mine, got)
    quarter = total // 4
    real_part = modulated[:, :half]
    imag_part = modulated[:, half:]
    freq = jnp.arange(half, dtype=jnp.int32) % MFREQ
    variants = []
    for u in range(4):
        step = (freq * u) % 4
        re_u = jnp.where(step == 0, real_part, jnp.where(step == 1, imag_part, jnp.where(step == 2, -real_part, -imag_part)))
        im_u = jnp.where(step == 0, imag_part, jnp.where(step == 1, -real_part, jnp.where(step == 2, -imag_part, real_part)))
        variants.append(jnp.concatenate([re_u, im_u], axis=1))
    stacked = jnp.concatenate(variants, axis=0)
    turned = rotate_all(refs_block.astype(jnp.float32), quarter, total)
    found = lax.dot_general(
        stacked, turned, (((1,), (1,)), ((), ())), preferred_element_type=jnp.float32
    )
    best = jnp.max(found.reshape(4, count, quarter, block), axis=(0, 2)) * (1.0 / math.sqrt(K))
    best_scores = lax.all_to_all(best, "rot", 0, 1, tiled=True)

    return (refs, best_scores)


def solution(mesh):
    in_specs = (P("dom", None), P("dom"), P("dom"), P("dom"), P())
    out_specs = (P("dom", None), P(("dom", "rot"), None))
    return jax.shard_map(local, mesh=mesh, in_specs=in_specs, out_specs=out_specs, check_vma=False)
```

```python
import math

import jax
import numpy as np
import jax.numpy as jnp
from jax import lax
from jax.experimental import pallas as pl
from jax.experimental.pallas import tpu as pltpu
from jax.sharding import PartitionSpec as P

CYCLES = 64
MFREQ = 64
CLS_DEV = 6
K = 8192


def split_dot(member, value):
    high = value.astype(jnp.bfloat16)
    rest = value - high.astype(jnp.float32)
    mid = rest.astype(jnp.bfloat16)
    low = (rest - mid.astype(jnp.float32)).astype(jnp.bfloat16)
    total = jnp.dot(member, high, preferred_element_type=jnp.float32)
    total = total + jnp.dot(member, mid, preferred_element_type=jnp.float32)
    return total + jnp.dot(member, low, preferred_element_type=jnp.float32)


def prologue_kernel(
    x_ref, cos_ref, sin_ref, rot_ref, group_ref, table_ref, assign_ref,
    pay_ref, mod_ref, w_ref, ctf_ref, cos_scr, sin_scr,
):
    count = x_ref.shape[0]
    block = pay_ref.shape[1]
    for p in range(count):
        ctf_ref[pl.ds(p, 1), :] = table_ref[pl.ds(group_ref[p], 1), :]
        cos_scr[pl.ds(p, 1), :] = cos_ref[pl.ds(rot_ref[p], 1), :]
        sin_scr[pl.ds(p, 1), :] = sin_ref[pl.ds(rot_ref[p], 1), :]
    first_class = lax.axis_index("rot") * block
    classes = first_class + lax.broadcasted_iota(jnp.int32, (block, count), 0)
    member = (classes == assign_ref[...]).astype(jnp.bfloat16)
    half = x_ref.shape[1] // 2
    lanes = cos_ref.shape[1]
    chunks, _, width = pay_ref.shape
    width -= ctf_ref.shape[1]
    cosine = cos_scr[...]
    sine = sin_scr[...]
    low = lax.broadcasted_iota(jnp.int32, cosine.shape, 1) < MFREQ
    for j in range(half // lanes):
        gain = jnp.where(low, ctf_ref[:, 2 * j : 2 * j + 1], ctf_ref[:, 2 * j + 1 : 2 * j + 2])
        re_cols = pl.ds(j * lanes, lanes)
        im_cols = pl.ds(half + j * lanes, lanes)
        real_part = x_ref[:, re_cols].astype(jnp.float32)
        imag_part = x_ref[:, im_cols].astype(jnp.float32)
        w_ref[:, re_cols] = (real_part * cosine + imag_part * sine) * gain
        w_ref[:, im_cols] = (imag_part * cosine - real_part * sine) * gain
        mod_ref[:, re_cols] = (real_part * gain).astype(jnp.bfloat16)
        mod_ref[:, im_cols] = (imag_part * gain).astype(jnp.bfloat16)
    gains = ctf_ref[...]
    denom = split_dot(member, gains * gains)
    numer = split_dot(member, w_ref[...])
    for x in range(chunks):
        pay_ref[x, :, :width] = numer[:, x * width : (x + 1) * width]
        pay_ref[x, :, width:] = denom


def derotate_and_sum(particles, rotation, group, ctf_table, assign, block, chunks, total):
    phase = (np.arange(2 * MFREQ)[None, :] % MFREQ) * np.arange(total)[:, None] % total
    angle = phase.astype(np.float32) * np.float32(2.0 * math.pi / total)
    count = particles.shape[0]
    smem = pl.BlockSpec(memory_space=pltpu.SMEM)
    vmem = pl.BlockSpec(memory_space=pltpu.VMEM)
    return pl.pallas_call(
        prologue_kernel,
        out_shape=(
            jax.ShapeDtypeStruct((chunks, block, K // chunks + CYCLES), jnp.float32),
            jax.ShapeDtypeStruct((count, K), jnp.bfloat16),
        ),
        in_specs=[vmem, vmem, vmem, smem, smem, vmem, vmem],
        scratch_shapes=[
            pltpu.VMEM((count, K), jnp.float32),
            pltpu.VMEM((count, ctf_table.shape[1]), jnp.float32),
            pltpu.VMEM((count, 2 * MFREQ), jnp.float32),
            pltpu.VMEM((count, 2 * MFREQ), jnp.float32),
        ],
    )(
        particles,
        jnp.asarray(np.cos(angle)),
        jnp.asarray(np.sin(angle)),
        rotation,
        group,
        ctf_table,
        assign.reshape(1, count),
    )


def rotate_all(refs, turns, total):
    count = refs.shape[0]
    half = K // 2
    real_part = refs[None, :, :half]
    imag_part = refs[None, :, half:]
    phase = (np.arange(half)[None, :] % MFREQ) * np.arange(turns)[:, None] % total
    angle = phase.astype(np.float32) * np.float32(2.0 * math.pi / total)
    cosine = jnp.asarray(np.cos(angle))[:, None, :]
    sine = jnp.asarray(np.sin(angle))[:, None, :]
    turned = jnp.concatenate(
        [real_part * cosine - imag_part * sine, real_part * sine + imag_part * cosine], axis=2
    )
    return turned.reshape(turns * count, K).astype(jnp.bfloat16)


def local(particles, assign, rot_index, group, ctf_table):
    dom_rank = lax.axis_index("dom")
    rot_count = lax.axis_size("rot")
    rot_rank = lax.axis_index("rot")
    dom_count = lax.axis_size("dom")
    classes = CLS_DEV * dom_count
    block = classes // rot_count
    owners_per_block = block // CLS_DEV
    total = 8 * rot_count
    count = particles.shape[0]

    half = K // 2
    chunks = dom_count
    width = K // chunks
    per_chunk = width // MFREQ
    payload, modulated = derotate_and_sum(
        particles, rot_index, group, ctf_table, assign, block, chunks, total
    )
    summed = jnp.sum(lax.all_to_all(payload, "dom", 0, 0, tiled=True), axis=0)
    numer_chunk = summed[:, :width].reshape(block, per_chunk, MFREQ)
    first_cycle = (dom_rank * per_chunk) % CYCLES
    denom_chunk = lax.dynamic_slice_in_dim(summed[:, width:], first_cycle, per_chunk, 1)
    plain_chunk = (numer_chunk / (denom_chunk[:, :, None] + 1.0)).reshape(block, width)
    plain = lax.all_to_all(
        jnp.broadcast_to(plain_chunk[None], (chunks, block, width)), "dom", 0, 0, tiled=True
    )
    plain = plain.transpose(1, 0, 2).reshape(block, K)
    spread = jnp.mean(plain * plain, axis=1)
    refs_f32 = plain / jnp.sqrt(spread + 1e-06)[:, None]
    refs_block = refs_f32.astype(jnp.bfloat16)

    others = rot_count - 1
    pairs = []
    for plane in range(rot_count):
        for sender in range(owners_per_block * others):
            owner = plane * owners_per_block + sender // others
            target = (plane + 1 + sender % others) % rot_count
            pairs.append((sender * rot_count + plane, owner * rot_count + target))
    sent = lax.dynamic_slice_in_dim(
        refs_block, jnp.minimum(dom_rank // others, owners_per_block - 1) * CLS_DEV, CLS_DEV, 0
    )
    got = lax.ppermute(sent, ("dom", "rot"), pairs)
    mine = lax.dynamic_slice_in_dim(refs_block, (dom_rank % owners_per_block) * CLS_DEV, CLS_DEV, 0)
    refs = jnp.where((dom_rank // owners_per_block) == rot_rank, mine, got)
    quarter = total // 4
    real_part = modulated[:, :half]
    imag_part = modulated[:, half:]
    freq = jnp.arange(half, dtype=jnp.int32) % MFREQ
    variants = []
    for u in range(4):
        step = (freq * u) % 4
        re_u = jnp.where(step == 0, real_part, jnp.where(step == 1, imag_part, jnp.where(step == 2, -real_part, -imag_part)))
        im_u = jnp.where(step == 0, imag_part, jnp.where(step == 1, -real_part, jnp.where(step == 2, -imag_part, real_part)))
        variants.append(jnp.concatenate([re_u, im_u], axis=1))
    stacked = jnp.concatenate(variants, axis=0)
    turned = rotate_all(refs_block.astype(jnp.float32), quarter, total)
    found = lax.dot_general(
        stacked, turned, (((1,), (1,)), ((), ())), preferred_element_type=jnp.float32
    )
    best = jnp.max(found.reshape(4, count, quarter, block), axis=(0, 2)) * (1.0 / math.sqrt(K))
    best_scores = lax.all_to_all(best, "rot", 0, 1, tiled=True)

    return (refs, best_scores)


def solution(mesh):
    in_specs = (P("dom", None), P("dom"), P("dom"), P("dom"), P())
    out_specs = (P("dom", None), P(("dom", "rot"), None))
    return jax.shard_map(local, mesh=mesh, in_specs=in_specs, out_specs=out_specs, check_vma=False)
```

```python
import math

import jax
import numpy as np
import jax.numpy as jnp
from jax import lax
from jax.experimental import pallas as pl
from jax.experimental.pallas import tpu as pltpu
from jax.sharding import PartitionSpec as P

CYCLES = 64
MFREQ = 64
CLS_DEV = 6
K = 8192


def column_angles(index, total, width):
    freqs = lax.broadcasted_iota(jnp.int32, (index.shape[0], width), 1) % MFREQ
    phase = freqs * index[:, None] % total
    return phase.astype(jnp.float32) * (2.0 * math.pi / total)


def split_dot(member, value):
    high = value.astype(jnp.bfloat16)
    rest = value - high.astype(jnp.float32)
    mid = rest.astype(jnp.bfloat16)
    low = (rest - mid.astype(jnp.float32)).astype(jnp.bfloat16)
    total = jnp.dot(member, high, preferred_element_type=jnp.float32)
    total = total + jnp.dot(member, mid, preferred_element_type=jnp.float32)
    return total + jnp.dot(member, low, preferred_element_type=jnp.float32)


def prologue_kernel(
    x_ref, cos_ref, sin_ref, rot_ref, group_ref, table_ref, assign_ref,
    pay_ref, mod_ref, w_ref, ctf_ref, cos_scr, sin_scr,
):
    count = x_ref.shape[0]
    block = pay_ref.shape[1]
    for p in range(count):
        ctf_ref[pl.ds(p, 1), :] = table_ref[pl.ds(group_ref[p], 1), :]
        cos_scr[pl.ds(p, 1), :] = cos_ref[pl.ds(rot_ref[p], 1), :]
        sin_scr[pl.ds(p, 1), :] = sin_ref[pl.ds(rot_ref[p], 1), :]
    first_class = lax.axis_index("rot") * block
    classes = first_class + lax.broadcasted_iota(jnp.int32, (block, count), 0)
    member = (classes == assign_ref[...]).astype(jnp.bfloat16)
    half = x_ref.shape[1] // 2
    lanes = cos_ref.shape[1]
    chunks, _, width = pay_ref.shape
    width -= ctf_ref.shape[1]
    cosine = cos_scr[...]
    sine = sin_scr[...]
    low = lax.broadcasted_iota(jnp.int32, cosine.shape, 1) < MFREQ
    for j in range(half // lanes):
        gain = jnp.where(low, ctf_ref[:, 2 * j : 2 * j + 1], ctf_ref[:, 2 * j + 1 : 2 * j + 2])
        re_cols = pl.ds(j * lanes, lanes)
        im_cols = pl.ds(half + j * lanes, lanes)
        real_part = x_ref[:, re_cols].astype(jnp.float32)
        imag_part = x_ref[:, im_cols].astype(jnp.float32)
        w_ref[:, re_cols] = (real_part * cosine + imag_part * sine) * gain
        w_ref[:, im_cols] = (imag_part * cosine - real_part * sine) * gain
        mod_ref[:, re_cols] = (real_part * gain).astype(jnp.bfloat16)
        mod_ref[:, im_cols] = (imag_part * gain).astype(jnp.bfloat16)
    gains = ctf_ref[...]
    denom = split_dot(member, gains * gains)
    numer = split_dot(member, w_ref[...])
    for x in range(chunks):
        pay_ref[x, :, :width] = numer[:, x * width : (x + 1) * width]
        pay_ref[x, :, width:] = denom


def derotate_and_sum(particles, rotation, group, ctf_table, assign, block, chunks, total):
    phase = (np.arange(2 * MFREQ)[None, :] % MFREQ) * np.arange(total)[:, None] % total
    angle = phase.astype(np.float32) * np.float32(2.0 * math.pi / total)
    count = particles.shape[0]
    smem = pl.BlockSpec(memory_space=pltpu.SMEM)
    vmem = pl.BlockSpec(memory_space=pltpu.VMEM)
    return pl.pallas_call(
        prologue_kernel,
        out_shape=(
            jax.ShapeDtypeStruct((chunks, block, K // chunks + CYCLES), jnp.float32),
            jax.ShapeDtypeStruct((count, K), jnp.bfloat16),
        ),
        in_specs=[vmem, vmem, vmem, smem, smem, vmem, vmem],
        scratch_shapes=[
            pltpu.VMEM((count, K), jnp.float32),
            pltpu.VMEM((count, ctf_table.shape[1]), jnp.float32),
            pltpu.VMEM((count, 2 * MFREQ), jnp.float32),
            pltpu.VMEM((count, 2 * MFREQ), jnp.float32),
        ],
    )(
        particles,
        jnp.asarray(np.cos(angle)),
        jnp.asarray(np.sin(angle)),
        rotation,
        group,
        ctf_table,
        assign.reshape(1, count),
    )


def rotate_all(refs, turns, total):
    count = refs.shape[0]
    half = K // 2
    real_part = refs[None, :, :half]
    imag_part = refs[None, :, half:]
    angle = column_angles(jnp.arange(turns, dtype=jnp.int32), total, half)
    cosine = jnp.cos(angle)[:, None, :]
    sine = jnp.sin(angle)[:, None, :]
    turned = jnp.concatenate(
        [real_part * cosine - imag_part * sine, real_part * sine + imag_part * cosine], axis=2
    )
    return turned.reshape(turns * count, K).astype(jnp.bfloat16)


def local(particles, assign, rot_index, group, ctf_table):
    dom_rank = lax.axis_index("dom")
    rot_count = lax.axis_size("rot")
    rot_rank = lax.axis_index("rot")
    dom_count = lax.axis_size("dom")
    classes = CLS_DEV * dom_count
    block = classes // rot_count
    owners_per_block = block // CLS_DEV
    total = 8 * rot_count
    count = particles.shape[0]

    half = K // 2
    chunks = dom_count
    width = K // chunks
    per_chunk = width // MFREQ
    payload, modulated = derotate_and_sum(
        particles, rot_index, group, ctf_table, assign, block, chunks, total
    )
    summed = jnp.sum(lax.all_to_all(payload, "dom", 0, 0, tiled=True), axis=0)
    numer_chunk = summed[:, :width].reshape(block, per_chunk, MFREQ)
    first_cycle = (dom_rank * per_chunk) % CYCLES
    denom_chunk = lax.dynamic_slice_in_dim(summed[:, width:], first_cycle, per_chunk, 1)
    plain_chunk = (numer_chunk / (denom_chunk[:, :, None] + 1.0)).reshape(block, width)
    plain = lax.all_to_all(
        jnp.broadcast_to(plain_chunk[None], (chunks, block, width)), "dom", 0, 0, tiled=True
    )
    plain = plain.transpose(1, 0, 2).reshape(block, K)
    spread = jnp.mean(plain * plain, axis=1)
    refs_f32 = plain / jnp.sqrt(spread + 1e-06)[:, None]
    refs_block = refs_f32.astype(jnp.bfloat16)

    others = rot_count - 1
    pairs = []
    for plane in range(rot_count):
        for sender in range(owners_per_block * others):
            owner = plane * owners_per_block + sender // others
            target = (plane + 1 + sender % others) % rot_count
            pairs.append((sender * rot_count + plane, owner * rot_count + target))
    sent = lax.dynamic_slice_in_dim(
        refs_block, jnp.minimum(dom_rank // others, owners_per_block - 1) * CLS_DEV, CLS_DEV, 0
    )
    flat = (CLS_DEV * 8, K // 8)
    got = lax.ppermute(sent.reshape(flat), ("dom", "rot"), pairs).reshape(sent.shape)
    mine = lax.dynamic_slice_in_dim(refs_block, (dom_rank % owners_per_block) * CLS_DEV, CLS_DEV, 0)
    refs = jnp.where((dom_rank // owners_per_block) == rot_rank, mine, got)
    quarter = total // 4
    real_part = modulated[:, :half]
    imag_part = modulated[:, half:]
    freq = jnp.arange(half, dtype=jnp.int32) % MFREQ
    variants = []
    for u in range(4):
        step = (freq * u) % 4
        re_u = jnp.where(step == 0, real_part, jnp.where(step == 1, imag_part, jnp.where(step == 2, -real_part, -imag_part)))
        im_u = jnp.where(step == 0, imag_part, jnp.where(step == 1, -real_part, jnp.where(step == 2, -imag_part, real_part)))
        variants.append(jnp.concatenate([re_u, im_u], axis=1))
    stacked = jnp.concatenate(variants, axis=0)
    turned = rotate_all(refs_block.astype(jnp.float32), quarter, total)
    found = lax.dot_general(
        stacked, turned, (((1,), (1,)), ((), ())), preferred_element_type=jnp.float32
    )
    best = jnp.max(found.reshape(4, count, quarter, block), axis=(0, 2)) * (1.0 / math.sqrt(K))
    best_scores = lax.all_to_all(best, "rot", 0, 1, tiled=True)

    return (refs, best_scores)


def solution(mesh):
    in_specs = (P("dom", None), P("dom"), P("dom"), P("dom"), P())
    out_specs = (P("dom", None), P(("dom", "rot"), None))
    return jax.shard_map(local, mesh=mesh, in_specs=in_specs, out_specs=out_specs, check_vma=False)
```

```python
import math

import jax
import numpy as np
import jax.numpy as jnp
from jax import lax
from jax.experimental import pallas as pl
from jax.experimental.pallas import tpu as pltpu
from jax.sharding import PartitionSpec as P

CYCLES = 64
MFREQ = 64
CLS_DEV = 6
K = 8192


def column_angles(index, total, width):
    freqs = lax.broadcasted_iota(jnp.int32, (index.shape[0], width), 1) % MFREQ
    phase = freqs * index[:, None] % total
    return phase.astype(jnp.float32) * (2.0 * math.pi / total)


def split_dot(member, value):
    high = value.astype(jnp.bfloat16)
    rest = value - high.astype(jnp.float32)
    mid = rest.astype(jnp.bfloat16)
    low = (rest - mid.astype(jnp.float32)).astype(jnp.bfloat16)
    total = jnp.dot(member, high, preferred_element_type=jnp.float32)
    total = total + jnp.dot(member, mid, preferred_element_type=jnp.float32)
    return total + jnp.dot(member, low, preferred_element_type=jnp.float32)


def prologue_kernel(
    x_ref, cos_ref, sin_ref, rot_ref, group_ref, table_ref, assign_ref,
    pay_ref, w_ref, ctf_ref, cos_scr, sin_scr,
):
    count = x_ref.shape[0]
    block = pay_ref.shape[1]
    for p in range(count):
        ctf_ref[pl.ds(p, 1), :] = table_ref[pl.ds(group_ref[p], 1), :]
        cos_scr[pl.ds(p, 1), :] = cos_ref[pl.ds(rot_ref[p], 1), :]
        sin_scr[pl.ds(p, 1), :] = sin_ref[pl.ds(rot_ref[p], 1), :]
    first_class = lax.axis_index("rot") * block
    classes = first_class + lax.broadcasted_iota(jnp.int32, (block, count), 0)
    member = (classes == assign_ref[...]).astype(jnp.bfloat16)
    half = x_ref.shape[1] // 2
    lanes = cos_ref.shape[1]
    chunks, _, width = pay_ref.shape
    width -= ctf_ref.shape[1]
    cosine = cos_scr[...]
    sine = sin_scr[...]
    low = lax.broadcasted_iota(jnp.int32, cosine.shape, 1) < MFREQ
    for j in range(half // lanes):
        gain = jnp.where(low, ctf_ref[:, 2 * j : 2 * j + 1], ctf_ref[:, 2 * j + 1 : 2 * j + 2])
        re_cols = pl.ds(j * lanes, lanes)
        im_cols = pl.ds(half + j * lanes, lanes)
        real_part = x_ref[:, re_cols].astype(jnp.float32)
        imag_part = x_ref[:, im_cols].astype(jnp.float32)
        w_ref[:, re_cols] = (real_part * cosine + imag_part * sine) * gain
        w_ref[:, im_cols] = (imag_part * cosine - real_part * sine) * gain
    gains = ctf_ref[...]
    denom = split_dot(member, gains * gains)
    numer = split_dot(member, w_ref[...])
    for x in range(chunks):
        pay_ref[x, :, :width] = numer[:, x * width : (x + 1) * width]
        pay_ref[x, :, width:] = denom


def derotate_and_sum(particles, rotation, group, ctf_table, assign, block, chunks, total):
    phase = (np.arange(2 * MFREQ)[None, :] % MFREQ) * np.arange(total)[:, None] % total
    angle = phase.astype(np.float32) * np.float32(2.0 * math.pi / total)
    count = particles.shape[0]
    smem = pl.BlockSpec(memory_space=pltpu.SMEM)
    vmem = pl.BlockSpec(memory_space=pltpu.VMEM)
    return pl.pallas_call(
        prologue_kernel,
        out_shape=jax.ShapeDtypeStruct((chunks, block, K // chunks + CYCLES), jnp.float32),
        in_specs=[vmem, vmem, vmem, smem, smem, vmem, vmem],
        scratch_shapes=[
            pltpu.VMEM((count, K), jnp.float32),
            pltpu.VMEM((count, ctf_table.shape[1]), jnp.float32),
            pltpu.VMEM((count, 2 * MFREQ), jnp.float32),
            pltpu.VMEM((count, 2 * MFREQ), jnp.float32),
        ],
    )(
        particles,
        jnp.asarray(np.cos(angle)),
        jnp.asarray(np.sin(angle)),
        rotation,
        group,
        ctf_table,
        assign.reshape(1, count),
    )


def rotate_all(refs, turns, total):
    count = refs.shape[0]
    half = K // 2
    real_part = refs[None, :, :half]
    imag_part = refs[None, :, half:]
    angle = column_angles(jnp.arange(turns, dtype=jnp.int32), total, half)
    cosine = jnp.cos(angle)[:, None, :]
    sine = jnp.sin(angle)[:, None, :]
    turned = jnp.concatenate(
        [real_part * cosine - imag_part * sine, real_part * sine + imag_part * cosine], axis=2
    )
    return turned.reshape(turns * count, K).astype(jnp.bfloat16)


def local(particles, assign, rot_index, group, ctf_table):
    dom_rank = lax.axis_index("dom")
    rot_count = lax.axis_size("rot")
    rot_rank = lax.axis_index("rot")
    dom_count = lax.axis_size("dom")
    classes = CLS_DEV * dom_count
    block = classes // rot_count
    owners_per_block = block // CLS_DEV
    total = 8 * rot_count
    count = particles.shape[0]

    half = K // 2
    chunks = dom_count
    width = K // chunks
    per_chunk = width // MFREQ
    payload = derotate_and_sum(
        particles, rot_index, group, ctf_table, assign, block, chunks, total
    )
    ctf_cols = jnp.repeat(ctf_table[group], MFREQ, axis=1)
    gain_cols = jnp.concatenate([ctf_cols, ctf_cols], axis=1)
    modulated = (particles.astype(jnp.float32) * gain_cols).astype(jnp.bfloat16)
    summed = jnp.sum(lax.all_to_all(payload, "dom", 0, 0, tiled=True), axis=0)
    numer_chunk = summed[:, :width].reshape(block, per_chunk, MFREQ)
    first_cycle = (dom_rank * per_chunk) % CYCLES
    denom_chunk = lax.dynamic_slice_in_dim(summed[:, width:], first_cycle, per_chunk, 1)
    plain_chunk = (numer_chunk / (denom_chunk[:, :, None] + 1.0)).reshape(block, width)
    plain = lax.all_to_all(
        jnp.broadcast_to(plain_chunk[None], (chunks, block, width)), "dom", 0, 0, tiled=True
    )
    plain = plain.transpose(1, 0, 2).reshape(block, K)
    spread = jnp.mean(plain * plain, axis=1)
    refs_f32 = plain / jnp.sqrt(spread + 1e-06)[:, None]
    refs_block = refs_f32.astype(jnp.bfloat16)

    others = rot_count - 1
    pairs = []
    for plane in range(rot_count):
        for sender in range(owners_per_block * others):
            owner = plane * owners_per_block + sender // others
            target = (plane + 1 + sender % others) % rot_count
            pairs.append((sender * rot_count + plane, owner * rot_count + target))
    sent = lax.dynamic_slice_in_dim(
        refs_block, jnp.minimum(dom_rank // others, owners_per_block - 1) * CLS_DEV, CLS_DEV, 0
    )
    got = lax.ppermute(sent, ("dom", "rot"), pairs)
    mine = lax.dynamic_slice_in_dim(refs_block, (dom_rank % owners_per_block) * CLS_DEV, CLS_DEV, 0)
    refs = jnp.where((dom_rank // owners_per_block) == rot_rank, mine, got)
    quarter = total // 4
    real_part = modulated[:, :half]
    imag_part = modulated[:, half:]
    freq = jnp.arange(half, dtype=jnp.int32) % MFREQ
    variants = []
    for u in range(4):
        step = (freq * u) % 4
        re_u = jnp.where(step == 0, real_part, jnp.where(step == 1, imag_part, jnp.where(step == 2, -real_part, -imag_part)))
        im_u = jnp.where(step == 0, imag_part, jnp.where(step == 1, -real_part, jnp.where(step == 2, -imag_part, real_part)))
        variants.append(jnp.concatenate([re_u, im_u], axis=1))
    stacked = jnp.concatenate(variants, axis=0)
    turned = rotate_all(refs_block.astype(jnp.float32), quarter, total)
    found = lax.dot_general(
        stacked, turned, (((1,), (1,)), ((), ())), preferred_element_type=jnp.float32
    )
    best = jnp.max(found.reshape(4, count, quarter, block), axis=(0, 2)) * (1.0 / math.sqrt(K))
    best_scores = lax.all_to_all(best, "rot", 0, 1, tiled=True)

    return (refs, best_scores)


def solution(mesh):
    in_specs = (P("dom", None), P("dom"), P("dom"), P("dom"), P())
    out_specs = (P("dom", None), P(("dom", "rot"), None))
    return jax.shard_map(local, mesh=mesh, in_specs=in_specs, out_specs=out_specs, check_vma=False)
```

```python
import math

import jax
import numpy as np
import jax.numpy as jnp
from jax import lax
from jax.experimental import pallas as pl
from jax.experimental.pallas import tpu as pltpu
from jax.sharding import PartitionSpec as P

CYCLES = 64
MFREQ = 64
CLS_DEV = 6
K = 8192


def column_angles(index, total, width):
    freqs = lax.broadcasted_iota(jnp.int32, (index.shape[0], width), 1) % MFREQ
    phase = freqs * index[:, None] % total
    return phase.astype(jnp.float32) * (2.0 * math.pi / total)


def split_dot(member, value):
    high = value.astype(jnp.bfloat16)
    rest = value - high.astype(jnp.float32)
    mid = rest.astype(jnp.bfloat16)
    low = (rest - mid.astype(jnp.float32)).astype(jnp.bfloat16)
    total = jnp.dot(member, high, preferred_element_type=jnp.float32)
    total = total + jnp.dot(member, mid, preferred_element_type=jnp.float32)
    return total + jnp.dot(member, low, preferred_element_type=jnp.float32)


def prologue_kernel(
    x_ref, cos_ref, sin_ref, rot_ref, group_ref, table_ref, assign_ref,
    pay_ref, mod_ref, w_ref, ctf_ref, cos_scr, sin_scr,
):
    count = x_ref.shape[0]
    block = pay_ref.shape[1]
    for p in range(count):
        ctf_ref[pl.ds(p, 1), :] = table_ref[pl.ds(group_ref[p], 1), :]
        cos_scr[pl.ds(p, 1), :] = cos_ref[pl.ds(rot_ref[p], 1), :]
        sin_scr[pl.ds(p, 1), :] = sin_ref[pl.ds(rot_ref[p], 1), :]
    first_class = lax.axis_index("rot") * block
    classes = first_class + lax.broadcasted_iota(jnp.int32, (block, count), 0)
    member = (classes == assign_ref[...]).astype(jnp.bfloat16)
    half = x_ref.shape[1] // 2
    lanes = cos_ref.shape[1]
    chunks, _, width = pay_ref.shape
    width -= ctf_ref.shape[1]
    cosine = cos_scr[...]
    sine = sin_scr[...]
    low = lax.broadcasted_iota(jnp.int32, cosine.shape, 1) < MFREQ
    for j in range(half // lanes):
        gain = jnp.where(low, ctf_ref[:, 2 * j : 2 * j + 1], ctf_ref[:, 2 * j + 1 : 2 * j + 2])
        re_cols = pl.ds(j * lanes, lanes)
        im_cols = pl.ds(half + j * lanes, lanes)
        real_part = x_ref[:, re_cols].astype(jnp.float32)
        imag_part = x_ref[:, im_cols].astype(jnp.float32)
        w_ref[:, re_cols] = (real_part * cosine + imag_part * sine) * gain
        w_ref[:, im_cols] = (imag_part * cosine - real_part * sine) * gain
        mod_ref[:, re_cols] = (real_part * gain).astype(jnp.bfloat16)
        mod_ref[:, im_cols] = (imag_part * gain).astype(jnp.bfloat16)
    gains = ctf_ref[...]
    denom = split_dot(member, gains * gains)
    numer = split_dot(member, w_ref[...])
    for x in range(chunks):
        pay_ref[x, :, :width] = numer[:, x * width : (x + 1) * width]
        pay_ref[x, :, width:] = denom


def derotate_and_sum(particles, rotation, group, ctf_table, assign, block, chunks, total):
    phase = (np.arange(2 * MFREQ)[None, :] % MFREQ) * np.arange(total)[:, None] % total
    angle = phase.astype(np.float32) * np.float32(2.0 * math.pi / total)
    count = particles.shape[0]
    smem = pl.BlockSpec(memory_space=pltpu.SMEM)
    vmem = pl.BlockSpec(memory_space=pltpu.VMEM)
    return pl.pallas_call(
        prologue_kernel,
        out_shape=(
            jax.ShapeDtypeStruct((chunks, block, K // chunks + CYCLES), jnp.float32),
            jax.ShapeDtypeStruct((count, K), jnp.bfloat16),
        ),
        in_specs=[vmem, vmem, vmem, smem, smem, vmem, vmem],
        scratch_shapes=[
            pltpu.VMEM((count, K), jnp.float32),
            pltpu.VMEM((count, ctf_table.shape[1]), jnp.float32),
            pltpu.VMEM((count, 2 * MFREQ), jnp.float32),
            pltpu.VMEM((count, 2 * MFREQ), jnp.float32),
        ],
    )(
        particles,
        jnp.asarray(np.cos(angle)),
        jnp.asarray(np.sin(angle)),
        rotation,
        group,
        ctf_table,
        assign.reshape(1, count),
    )


def score_kernel(x_ref, refs_ref, cos_ref, sin_ref, out_ref, turned_scr, found_scr):
    block = refs_ref.shape[0]
    turns, half = cos_ref.shape
    count = out_ref.shape[0]
    real_part = refs_ref[:, :half]
    imag_part = refs_ref[:, half:]
    for r in range(turns):
        cosine = cos_ref[pl.ds(r, 1), :]
        sine = sin_ref[pl.ds(r, 1), :]
        rows = pl.ds(r * block, block)
        turned_scr[rows, :half] = (real_part * cosine - imag_part * sine).astype(jnp.bfloat16)
        turned_scr[rows, half:] = (real_part * sine + imag_part * cosine).astype(jnp.bfloat16)
    found = lax.dot_general(
        x_ref[...], turned_scr[...], (((1,), (1,)), ((), ())), preferred_element_type=jnp.float32
    )
    best = found[:count]
    for u in range(1, x_ref.shape[0] // count):
        best = jnp.maximum(best, found[u * count : (u + 1) * count])
    found_scr[...] = best
    top = found_scr[:, pl.ds(0, block)]
    for r in range(1, turns):
        top = jnp.maximum(top, found_scr[:, pl.ds(r * block, block)])
    out_ref[...] = top * (1.0 / math.sqrt(K))


def score_all(stacked, refs, turns, total):
    block = refs.shape[0]
    half = K // 2
    phase = (np.arange(half)[None, :] % MFREQ) * np.arange(turns)[:, None] % total
    angle = phase.astype(np.float32) * np.float32(2.0 * math.pi / total)
    count = stacked.shape[0] // 4
    return pl.pallas_call(
        score_kernel,
        out_shape=jax.ShapeDtypeStruct((count, block), jnp.float32),
        scratch_shapes=[
            pltpu.VMEM((turns * block, K), jnp.bfloat16),
            pltpu.VMEM((count, turns * block), jnp.float32),
        ],
    )(stacked, refs, jnp.asarray(np.cos(angle)), jnp.asarray(np.sin(angle)))


def local(particles, assign, rot_index, group, ctf_table):
    dom_rank = lax.axis_index("dom")
    rot_count = lax.axis_size("rot")
    rot_rank = lax.axis_index("rot")
    dom_count = lax.axis_size("dom")
    classes = CLS_DEV * dom_count
    block = classes // rot_count
    owners_per_block = block // CLS_DEV
    total = 8 * rot_count
    count = particles.shape[0]

    half = K // 2
    chunks = dom_count
    width = K // chunks
    per_chunk = width // MFREQ
    payload, modulated = derotate_and_sum(
        particles, rot_index, group, ctf_table, assign, block, chunks, total
    )
    summed = jnp.sum(lax.all_to_all(payload, "dom", 0, 0, tiled=True), axis=0)
    numer_chunk = summed[:, :width].reshape(block, per_chunk, MFREQ)
    first_cycle = (dom_rank * per_chunk) % CYCLES
    denom_chunk = lax.dynamic_slice_in_dim(summed[:, width:], first_cycle, per_chunk, 1)
    plain_chunk = (numer_chunk / (denom_chunk[:, :, None] + 1.0)).reshape(block, width)
    plain = lax.all_to_all(
        jnp.broadcast_to(plain_chunk[None], (chunks, block, width)), "dom", 0, 0, tiled=True
    )
    plain = plain.transpose(1, 0, 2).reshape(block, K)
    spread = jnp.mean(plain * plain, axis=1)
    refs_f32 = plain / jnp.sqrt(spread + 1e-06)[:, None]
    refs_block = refs_f32.astype(jnp.bfloat16)

    others = rot_count - 1
    pairs = []
    for plane in range(rot_count):
        for sender in range(owners_per_block * others):
            owner = plane * owners_per_block + sender // others
            target = (plane + 1 + sender % others) % rot_count
            pairs.append((sender * rot_count + plane, owner * rot_count + target))
    sent = lax.dynamic_slice_in_dim(
        refs_block, jnp.minimum(dom_rank // others, owners_per_block - 1) * CLS_DEV, CLS_DEV, 0
    )
    got = lax.ppermute(sent, ("dom", "rot"), pairs)
    mine = lax.dynamic_slice_in_dim(refs_block, (dom_rank % owners_per_block) * CLS_DEV, CLS_DEV, 0)
    refs = jnp.where((dom_rank // owners_per_block) == rot_rank, mine, got)
    quarter = total // 4
    real_part = modulated[:, :half]
    imag_part = modulated[:, half:]
    freq = jnp.arange(half, dtype=jnp.int32) % MFREQ
    variants = []
    for u in range(4):
        step = (freq * u) % 4
        re_u = jnp.where(step == 0, real_part, jnp.where(step == 1, imag_part, jnp.where(step == 2, -real_part, -imag_part)))
        im_u = jnp.where(step == 0, imag_part, jnp.where(step == 1, -real_part, jnp.where(step == 2, -imag_part, real_part)))
        variants.append(jnp.concatenate([re_u, im_u], axis=1))
    stacked = jnp.concatenate(variants, axis=0)
    best = score_all(stacked, refs_block.astype(jnp.float32), quarter, total)
    best_scores = lax.all_to_all(best, "rot", 0, 1, tiled=True)

    return (refs, best_scores)


def solution(mesh):
    in_specs = (P("dom", None), P("dom"), P("dom"), P("dom"), P())
    out_specs = (P("dom", None), P(("dom", "rot"), None))
    return jax.shard_map(local, mesh=mesh, in_specs=in_specs, out_specs=out_specs, check_vma=False)
```

```python
import math

import jax
import numpy as np
import jax.numpy as jnp
from jax import lax
from jax.experimental import pallas as pl
from jax.experimental.pallas import tpu as pltpu
from jax.sharding import PartitionSpec as P

CYCLES = 64
MFREQ = 64
CLS_DEV = 6
K = 8192


def column_angles(index, total, width):
    freqs = lax.broadcasted_iota(jnp.int32, (index.shape[0], width), 1) % MFREQ
    phase = freqs * index[:, None] % total
    return phase.astype(jnp.float32) * (2.0 * math.pi / total)


def split_dot(member, value):
    high = value.astype(jnp.bfloat16)
    rest = value - high.astype(jnp.float32)
    mid = rest.astype(jnp.bfloat16)
    low = (rest - mid.astype(jnp.float32)).astype(jnp.bfloat16)
    total = jnp.dot(member, high, preferred_element_type=jnp.float32)
    total = total + jnp.dot(member, mid, preferred_element_type=jnp.float32)
    return total + jnp.dot(member, low, preferred_element_type=jnp.float32)


def prologue_kernel(
    x_ref, cos_ref, sin_ref, rot_ref, group_ref, table_ref, assign_ref,
    pay_ref, mod_ref, w_ref, ctf_ref, cos_scr, sin_scr,
):
    count = x_ref.shape[0]
    block = pay_ref.shape[1]
    for p in range(count):
        ctf_ref[pl.ds(p, 1), :] = table_ref[pl.ds(group_ref[p], 1), :]
        cos_scr[pl.ds(p, 1), :] = cos_ref[pl.ds(rot_ref[p], 1), :]
        sin_scr[pl.ds(p, 1), :] = sin_ref[pl.ds(rot_ref[p], 1), :]
    first_class = lax.axis_index("rot") * block
    classes = first_class + lax.broadcasted_iota(jnp.int32, (block, count), 0)
    member = (classes == assign_ref[...]).astype(jnp.bfloat16)
    half = x_ref.shape[1] // 2
    lanes = cos_ref.shape[1]
    chunks, _, width = pay_ref.shape
    width -= ctf_ref.shape[1]
    cosine = cos_scr[...]
    sine = sin_scr[...]
    low = lax.broadcasted_iota(jnp.int32, cosine.shape, 1) < MFREQ
    for j in range(half // lanes):
        gain = jnp.where(low, ctf_ref[:, 2 * j : 2 * j + 1], ctf_ref[:, 2 * j + 1 : 2 * j + 2])
        re_cols = pl.ds(j * lanes, lanes)
        im_cols = pl.ds(half + j * lanes, lanes)
        real_part = x_ref[:, re_cols].astype(jnp.float32)
        imag_part = x_ref[:, im_cols].astype(jnp.float32)
        w_ref[:, re_cols] = (real_part * cosine + imag_part * sine) * gain
        w_ref[:, im_cols] = (imag_part * cosine - real_part * sine) * gain
        mod_ref[:, re_cols] = (real_part * gain).astype(jnp.bfloat16)
        mod_ref[:, im_cols] = (imag_part * gain).astype(jnp.bfloat16)
    gains = ctf_ref[...]
    denom = split_dot(member, gains * gains)
    numer = split_dot(member, w_ref[...])
    for x in range(chunks):
        pay_ref[x, :, :width] = numer[:, x * width : (x + 1) * width]
        pay_ref[x, :, width:] = denom


def derotate_and_sum(particles, rotation, group, ctf_table, assign, block, chunks, total):
    phase = (np.arange(2 * MFREQ)[None, :] % MFREQ) * np.arange(total)[:, None] % total
    angle = phase.astype(np.float32) * np.float32(2.0 * math.pi / total)
    count = particles.shape[0]
    smem = pl.BlockSpec(memory_space=pltpu.SMEM)
    vmem = pl.BlockSpec(memory_space=pltpu.VMEM)
    return pl.pallas_call(
        prologue_kernel,
        out_shape=(
            jax.ShapeDtypeStruct((chunks, block, K // chunks + CYCLES), jnp.float32),
            jax.ShapeDtypeStruct((count, K), jnp.bfloat16),
        ),
        in_specs=[vmem, vmem, vmem, smem, smem, vmem, vmem],
        scratch_shapes=[
            pltpu.VMEM((count, K), jnp.float32),
            pltpu.VMEM((count, ctf_table.shape[1]), jnp.float32),
            pltpu.VMEM((count, 2 * MFREQ), jnp.float32),
            pltpu.VMEM((count, 2 * MFREQ), jnp.float32),
        ],
    )(
        particles,
        jnp.asarray(np.cos(angle)),
        jnp.asarray(np.sin(angle)),
        rotation,
        group,
        ctf_table,
        assign.reshape(1, count),
    )


def rotate_all(refs, turns, total):
    count = refs.shape[0]
    half = K // 2
    real_part = refs[None, :, :half]
    imag_part = refs[None, :, half:]
    angle = column_angles(jnp.arange(turns, dtype=jnp.int32), total, half)
    cosine = jnp.cos(angle)[:, None, :]
    sine = jnp.sin(angle)[:, None, :]
    turned = jnp.concatenate(
        [real_part * cosine - imag_part * sine, real_part * sine + imag_part * cosine], axis=2
    )
    return turned.reshape(turns * count, K).astype(jnp.bfloat16)


def local(particles, assign, rot_index, group, ctf_table):
    dom_rank = lax.axis_index("dom")
    rot_count = lax.axis_size("rot")
    rot_rank = lax.axis_index("rot")
    dom_count = lax.axis_size("dom")
    classes = CLS_DEV * dom_count
    block = classes // rot_count
    owners_per_block = block // CLS_DEV
    total = 8 * rot_count
    count = particles.shape[0]

    half = K // 2
    chunks = dom_count
    width = K // chunks
    per_chunk = width // MFREQ
    payload, modulated = derotate_and_sum(
        particles, rot_index, group, ctf_table, assign, block, chunks, total
    )
    summed = jnp.sum(lax.all_to_all(payload, "dom", 0, 0, tiled=True), axis=0)
    numer_chunk = summed[:, :width].reshape(block, per_chunk, MFREQ)
    first_cycle = (dom_rank * per_chunk) % CYCLES
    denom_chunk = lax.dynamic_slice_in_dim(summed[:, width:], first_cycle, per_chunk, 1)
    plain_chunk = (numer_chunk / (denom_chunk[:, :, None] + 1.0)).reshape(block, width)
    plain = lax.all_to_all(
        jnp.broadcast_to(plain_chunk[None], (chunks, block, width)), "dom", 0, 0, tiled=True
    )
    plain = plain.transpose(1, 0, 2).reshape(block, K)
    spread = jnp.mean(plain * plain, axis=1)
    refs_f32 = plain / jnp.sqrt(spread + 1e-06)[:, None]
    refs_block = refs_f32.astype(jnp.bfloat16)

    others = rot_count - 1
    pairs = []
    for plane in range(rot_count):
        first_owner = plane * owners_per_block
        senders = [x for x in range(dom_count) if x // owners_per_block != plane]
        for owner in range(first_owner, first_owner + owners_per_block):
            pairs.append((owner * rot_count + plane, owner * rot_count + plane))
        for idx, sender in enumerate(senders[: owners_per_block * others]):
            owner = first_owner + idx // others
            target = (plane + 1 + idx % others) % rot_count
            pairs.append((sender * rot_count + plane, owner * rot_count + target))
    own_plane = (dom_rank // owners_per_block) == rot_rank
    idx = jnp.where(dom_rank > rot_rank * owners_per_block, dom_rank - owners_per_block, dom_rank)
    slot = jnp.where(own_plane, dom_rank % owners_per_block, jnp.minimum(idx // others, owners_per_block - 1))
    sent = lax.dynamic_slice_in_dim(refs_block, slot * CLS_DEV, CLS_DEV, 0)
    refs = lax.ppermute(sent, ("dom", "rot"), pairs)
    quarter = total // 4
    real_part = modulated[:, :half]
    imag_part = modulated[:, half:]
    freq = jnp.arange(half, dtype=jnp.int32) % MFREQ
    variants = []
    for u in range(4):
        step = (freq * u) % 4
        re_u = jnp.where(step == 0, real_part, jnp.where(step == 1, imag_part, jnp.where(step == 2, -real_part, -imag_part)))
        im_u = jnp.where(step == 0, imag_part, jnp.where(step == 1, -real_part, jnp.where(step == 2, -imag_part, real_part)))
        variants.append(jnp.concatenate([re_u, im_u], axis=1))
    stacked = jnp.concatenate(variants, axis=0)
    turned = rotate_all(refs_block.astype(jnp.float32), quarter, total)
    found = lax.dot_general(
        stacked, turned, (((1,), (1,)), ((), ())), preferred_element_type=jnp.float32
    )
    best = jnp.max(found.reshape(4, count, quarter, block), axis=(0, 2)) * (1.0 / math.sqrt(K))
    best_scores = lax.all_to_all(best, "rot", 0, 1, tiled=True)

    return (refs, best_scores)


def solution(mesh):
    in_specs = (P("dom", None), P("dom"), P("dom"), P("dom"), P())
    out_specs = (P("dom", None), P(("dom", "rot"), None))
    return jax.shard_map(local, mesh=mesh, in_specs=in_specs, out_specs=out_specs, check_vma=False)
```

```python
import math

import jax
import numpy as np
import jax.numpy as jnp
from jax import lax
from jax.experimental import pallas as pl
from jax.experimental.pallas import tpu as pltpu
from jax.sharding import PartitionSpec as P

CYCLES = 64
MFREQ = 64
CLS_DEV = 6
K = 8192


def column_angles(index, total, width):
    freqs = lax.broadcasted_iota(jnp.int32, (index.shape[0], width), 1) % MFREQ
    phase = freqs * index[:, None] % total
    return phase.astype(jnp.float32) * (2.0 * math.pi / total)


def split_dot(member, value):
    high = value.astype(jnp.bfloat16)
    rest = value - high.astype(jnp.float32)
    mid = rest.astype(jnp.bfloat16)
    low = (rest - mid.astype(jnp.float32)).astype(jnp.bfloat16)
    total = jnp.dot(member, high, preferred_element_type=jnp.float32)
    total = total + jnp.dot(member, mid, preferred_element_type=jnp.float32)
    return total + jnp.dot(member, low, preferred_element_type=jnp.float32)


def prologue_kernel(
    x_ref, cos_ref, sin_ref, rot_ref, group_ref, table_ref, assign_ref,
    pay_ref, mod_ref, w_ref, ctf_ref, cos_scr, sin_scr,
):
    count = x_ref.shape[0]
    block = pay_ref.shape[1] - 8
    for p in range(count):
        ctf_ref[pl.ds(p, 1), :] = table_ref[pl.ds(group_ref[p], 1), :]
        cos_scr[pl.ds(p, 1), :] = cos_ref[pl.ds(rot_ref[p], 1), :]
        sin_scr[pl.ds(p, 1), :] = sin_ref[pl.ds(rot_ref[p], 1), :]
    first_class = lax.axis_index("rot") * block
    classes = first_class + lax.broadcasted_iota(jnp.int32, (block, count), 0)
    member = (classes == assign_ref[...]).astype(jnp.bfloat16)
    half = x_ref.shape[1] // 2
    lanes = cos_ref.shape[1]
    chunks, _, width = pay_ref.shape
    cosine = cos_scr[...]
    sine = sin_scr[...]
    low = lax.broadcasted_iota(jnp.int32, cosine.shape, 1) < MFREQ
    for j in range(half // lanes):
        gain = jnp.where(low, ctf_ref[:, 2 * j : 2 * j + 1], ctf_ref[:, 2 * j + 1 : 2 * j + 2])
        re_cols = pl.ds(j * lanes, lanes)
        im_cols = pl.ds(half + j * lanes, lanes)
        real_part = x_ref[:, re_cols].astype(jnp.float32)
        imag_part = x_ref[:, im_cols].astype(jnp.float32)
        w_ref[:, re_cols] = (real_part * cosine + imag_part * sine) * gain
        w_ref[:, im_cols] = (imag_part * cosine - real_part * sine) * gain
        mod_ref[:, re_cols] = (real_part * gain).astype(jnp.bfloat16)
        mod_ref[:, im_cols] = (imag_part * gain).astype(jnp.bfloat16)
    gains = ctf_ref[...]
    denom_t = split_dot(member, gains * gains).T
    numer = split_dot(member, w_ref[...])
    per_chunk = width // MFREQ
    cycles = gains.shape[1]
    for x in range(chunks):
        pay_ref[x, :block, :] = numer[:, x * width : (x + 1) * width]
        first = (x * per_chunk) % cycles
        pay_ref[x, block:, :] = jnp.zeros((pay_ref.shape[1] - block, width), jnp.float32)
        pay_ref[x, block : block + per_chunk, :block] = denom_t[first : first + per_chunk, :]


def derotate_and_sum(particles, rotation, group, ctf_table, assign, block, chunks, total):
    phase = (np.arange(2 * MFREQ)[None, :] % MFREQ) * np.arange(total)[:, None] % total
    angle = phase.astype(np.float32) * np.float32(2.0 * math.pi / total)
    count = particles.shape[0]
    smem = pl.BlockSpec(memory_space=pltpu.SMEM)
    vmem = pl.BlockSpec(memory_space=pltpu.VMEM)
    return pl.pallas_call(
        prologue_kernel,
        out_shape=(
            jax.ShapeDtypeStruct((chunks, block + 8, K // chunks), jnp.float32),
            jax.ShapeDtypeStruct((count, K), jnp.bfloat16),
        ),
        in_specs=[vmem, vmem, vmem, smem, smem, vmem, vmem],
        scratch_shapes=[
            pltpu.VMEM((count, K), jnp.float32),
            pltpu.VMEM((count, ctf_table.shape[1]), jnp.float32),
            pltpu.VMEM((count, 2 * MFREQ), jnp.float32),
            pltpu.VMEM((count, 2 * MFREQ), jnp.float32),
        ],
    )(
        particles,
        jnp.asarray(np.cos(angle)),
        jnp.asarray(np.sin(angle)),
        rotation,
        group,
        ctf_table,
        assign.reshape(1, count),
    )


def rotate_all(refs, turns, total):
    count = refs.shape[0]
    half = K // 2
    real_part = refs[None, :, :half]
    imag_part = refs[None, :, half:]
    angle = column_angles(jnp.arange(turns, dtype=jnp.int32), total, half)
    cosine = jnp.cos(angle)[:, None, :]
    sine = jnp.sin(angle)[:, None, :]
    turned = jnp.concatenate(
        [real_part * cosine - imag_part * sine, real_part * sine + imag_part * cosine], axis=2
    )
    return turned.reshape(turns * count, K).astype(jnp.bfloat16)


def local(particles, assign, rot_index, group, ctf_table):
    dom_rank = lax.axis_index("dom")
    rot_count = lax.axis_size("rot")
    rot_rank = lax.axis_index("rot")
    dom_count = lax.axis_size("dom")
    classes = CLS_DEV * dom_count
    block = classes // rot_count
    owners_per_block = block // CLS_DEV
    total = 8 * rot_count
    count = particles.shape[0]

    half = K // 2
    chunks = dom_count
    width = K // chunks
    per_chunk = width // MFREQ
    payload, modulated = derotate_and_sum(
        particles, rot_index, group, ctf_table, assign, block, chunks, total
    )
    summed = jnp.sum(lax.all_to_all(payload, "dom", 0, 0, tiled=True), axis=0)
    numer_chunk = summed[:block].reshape(block, per_chunk, MFREQ)
    denom_chunk = summed[block : block + per_chunk, :block].T
    plain_chunk = (numer_chunk / (denom_chunk[:, :, None] + 1.0)).reshape(block, width)
    plain = lax.all_to_all(
        jnp.broadcast_to(plain_chunk[None], (chunks, block, width)), "dom", 0, 0, tiled=True
    )
    plain = plain.transpose(1, 0, 2).reshape(block, K)
    spread = jnp.mean(plain * plain, axis=1)
    refs_f32 = plain / jnp.sqrt(spread + 1e-06)[:, None]
    refs_block = refs_f32.astype(jnp.bfloat16)

    others = rot_count - 1
    pairs = []
    for plane in range(rot_count):
        first_owner = plane * owners_per_block
        senders = [x for x in range(dom_count) if x // owners_per_block != plane]
        for owner in range(first_owner, first_owner + owners_per_block):
            pairs.append((owner * rot_count + plane, owner * rot_count + plane))
        for idx, sender in enumerate(senders[: owners_per_block * others]):
            owner = first_owner + idx // others
            target = (plane + 1 + idx % others) % rot_count
            pairs.append((sender * rot_count + plane, owner * rot_count + target))
    own_plane = (dom_rank // owners_per_block) == rot_rank
    idx = jnp.where(dom_rank > rot_rank * owners_per_block, dom_rank - owners_per_block, dom_rank)
    slot = jnp.where(own_plane, dom_rank % owners_per_block, jnp.minimum(idx // others, owners_per_block - 1))
    sent = lax.dynamic_slice_in_dim(refs_block, slot * CLS_DEV, CLS_DEV, 0)
    refs = lax.ppermute(sent, ("dom", "rot"), pairs)
    quarter = total // 4
    real_part = modulated[:, :half]
    imag_part = modulated[:, half:]
    freq = jnp.arange(half, dtype=jnp.int32) % MFREQ
    variants = []
    for u in range(4):
        step = (freq * u) % 4
        re_u = jnp.where(step == 0, real_part, jnp.where(step == 1, imag_part, jnp.where(step == 2, -real_part, -imag_part)))
        im_u = jnp.where(step == 0, imag_part, jnp.where(step == 1, -real_part, jnp.where(step == 2, -imag_part, real_part)))
        variants.append(jnp.concatenate([re_u, im_u], axis=1))
    stacked = jnp.concatenate(variants, axis=0)
    turned = rotate_all(refs_block.astype(jnp.float32), quarter, total)
    found = lax.dot_general(
        stacked, turned, (((1,), (1,)), ((), ())), preferred_element_type=jnp.float32
    )
    best = jnp.max(found.reshape(4, count, quarter, block), axis=(0, 2)) * (1.0 / math.sqrt(K))
    best_scores = lax.all_to_all(best, "rot", 0, 1, tiled=True)

    return (refs, best_scores)


def solution(mesh):
    in_specs = (P("dom", None), P("dom"), P("dom"), P("dom"), P())
    out_specs = (P("dom", None), P(("dom", "rot"), None))
    return jax.shard_map(local, mesh=mesh, in_specs=in_specs, out_specs=out_specs, check_vma=False)
```

```python
import math

import jax
import numpy as np
import jax.numpy as jnp
from jax import lax
from jax.experimental import pallas as pl
from jax.experimental.pallas import tpu as pltpu
from jax.sharding import PartitionSpec as P

CYCLES = 64
MFREQ = 64
CLS_DEV = 6
K = 8192


def column_angles(index, total, width):
    freqs = lax.broadcasted_iota(jnp.int32, (index.shape[0], width), 1) % MFREQ
    phase = freqs * index[:, None] % total
    return phase.astype(jnp.float32) * (2.0 * math.pi / total)


def split_dot(member, value):
    high = value.astype(jnp.bfloat16)
    rest = value - high.astype(jnp.float32)
    mid = rest.astype(jnp.bfloat16)
    low = (rest - mid.astype(jnp.float32)).astype(jnp.bfloat16)
    total = jnp.dot(member, high, preferred_element_type=jnp.float32)
    total = total + jnp.dot(member, mid, preferred_element_type=jnp.float32)
    return total + jnp.dot(member, low, preferred_element_type=jnp.float32)


def prologue_kernel(
    x_ref, cos_ref, sin_ref, rot_ref, group_ref, table_ref, assign_ref,
    pay_ref, mod_ref, w_ref, ctf_ref, cos_scr, sin_scr,
):
    count = x_ref.shape[0]
    block = pay_ref.shape[1]
    for p in range(count):
        ctf_ref[pl.ds(p, 1), :] = table_ref[pl.ds(group_ref[p], 1), :]
        cos_scr[pl.ds(p, 1), :] = cos_ref[pl.ds(rot_ref[p], 1), :]
        sin_scr[pl.ds(p, 1), :] = sin_ref[pl.ds(rot_ref[p], 1), :]
    first_class = lax.axis_index("rot") * block
    classes = first_class + lax.broadcasted_iota(jnp.int32, (block, count), 0)
    member = (classes == assign_ref[...]).astype(jnp.bfloat16)
    half = x_ref.shape[1] // 2
    lanes = cos_ref.shape[1]
    chunks, _, width = pay_ref.shape
    width -= ctf_ref.shape[1]
    cosine = cos_scr[...]
    sine = sin_scr[...]
    low = lax.broadcasted_iota(jnp.int32, cosine.shape, 1) < MFREQ
    for j in range(half // lanes):
        gain = jnp.where(low, ctf_ref[:, 2 * j : 2 * j + 1], ctf_ref[:, 2 * j + 1 : 2 * j + 2])
        re_cols = pl.ds(j * lanes, lanes)
        im_cols = pl.ds(half + j * lanes, lanes)
        real_part = x_ref[:, re_cols].astype(jnp.float32)
        imag_part = x_ref[:, im_cols].astype(jnp.float32)
        w_ref[:, re_cols] = (real_part * cosine + imag_part * sine) * gain
        w_ref[:, im_cols] = (imag_part * cosine - real_part * sine) * gain
        mod_ref[:, re_cols] = (real_part * gain).astype(jnp.bfloat16)
        mod_ref[:, im_cols] = (imag_part * gain).astype(jnp.bfloat16)
    gains = ctf_ref[...]
    denom = split_dot(member, gains * gains)
    numer = split_dot(member, w_ref[...])
    for x in range(chunks):
        pay_ref[x, :, :width] = numer[:, x * width : (x + 1) * width]
        pay_ref[x, :, width:] = denom


def derotate_and_sum(particles, rotation, group, ctf_table, assign, block, chunks, total):
    phase = (np.arange(2 * MFREQ)[None, :] % MFREQ) * np.arange(total)[:, None] % total
    angle = phase.astype(np.float32) * np.float32(2.0 * math.pi / total)
    count = particles.shape[0]
    smem = pl.BlockSpec(memory_space=pltpu.SMEM)
    vmem = pl.BlockSpec(memory_space=pltpu.VMEM)
    return pl.pallas_call(
        prologue_kernel,
        out_shape=(
            jax.ShapeDtypeStruct((chunks, block, K // chunks + CYCLES), jnp.float32),
            jax.ShapeDtypeStruct((count, K), jnp.bfloat16),
        ),
        in_specs=[vmem, vmem, vmem, smem, smem, vmem, vmem],
        scratch_shapes=[
            pltpu.VMEM((count, K), jnp.float32),
            pltpu.VMEM((count, ctf_table.shape[1]), jnp.float32),
            pltpu.VMEM((count, 2 * MFREQ), jnp.float32),
            pltpu.VMEM((count, 2 * MFREQ), jnp.float32),
        ],
    )(
        particles,
        jnp.asarray(np.cos(angle)),
        jnp.asarray(np.sin(angle)),
        rotation,
        group,
        ctf_table,
        assign.reshape(1, count),
    )


def rotate_all(refs, turns, total):
    count = refs.shape[0]
    half = K // 2
    real_part = refs[None, :, :half]
    imag_part = refs[None, :, half:]
    angle = column_angles(jnp.arange(turns, dtype=jnp.int32), total, half)
    cosine = jnp.cos(angle)[:, None, :]
    sine = jnp.sin(angle)[:, None, :]
    turned = jnp.concatenate(
        [real_part * cosine - imag_part * sine, real_part * sine + imag_part * cosine], axis=2
    )
    return turned.reshape(turns * count, K).astype(jnp.bfloat16)


def local(particles, assign, rot_index, group, ctf_table):
    dom_rank = lax.axis_index("dom")
    rot_count = lax.axis_size("rot")
    rot_rank = lax.axis_index("rot")
    dom_count = lax.axis_size("dom")
    classes = CLS_DEV * dom_count
    block = classes // rot_count
    owners_per_block = block // CLS_DEV
    total = 8 * rot_count
    count = particles.shape[0]

    half = K // 2
    chunks = dom_count
    width = K // chunks
    per_chunk = width // MFREQ
    payload, modulated = derotate_and_sum(
        particles, rot_index, group, ctf_table, assign, block, chunks, total
    )
    summed = jnp.sum(lax.all_to_all(payload, "dom", 0, 0, tiled=True), axis=0)
    numer_chunk = summed[:, :width].reshape(block, per_chunk, MFREQ)
    first_cycle = (dom_rank * per_chunk) % CYCLES
    denom_chunk = lax.dynamic_slice_in_dim(summed[:, width:], first_cycle, per_chunk, 1)
    plain_chunk = (numer_chunk / (denom_chunk[:, :, None] + 1.0)).reshape(block, width)
    plain = lax.all_to_all(
        jnp.broadcast_to(plain_chunk[None], (chunks, block, width)), "dom", 0, 0, tiled=True
    )
    plain = plain.transpose(1, 0, 2).reshape(block, K)
    spread = jnp.mean(plain * plain, axis=1)
    refs_f32 = plain / jnp.sqrt(spread + 1e-06)[:, None]
    refs_block = refs_f32.astype(jnp.bfloat16)

    others = rot_count - 1
    pairs = []
    for plane in range(rot_count):
        first_owner = plane * owners_per_block
        senders = [x for x in range(dom_count) if x // owners_per_block != plane]
        for owner in range(first_owner, first_owner + owners_per_block):
            pairs.append((owner * rot_count + plane, owner * rot_count + plane))
        for idx, sender in enumerate(senders[: owners_per_block * others]):
            owner = first_owner + idx // others
            target = (plane + 1 + idx % others) % rot_count
            pairs.append((sender * rot_count + plane, owner * rot_count + target))
    own_plane = (dom_rank // owners_per_block) == rot_rank
    idx = jnp.where(dom_rank > rot_rank * owners_per_block, dom_rank - owners_per_block, dom_rank)
    slot = jnp.where(own_plane, dom_rank % owners_per_block, jnp.minimum(idx // others, owners_per_block - 1))
    sent = lax.dynamic_slice_in_dim(refs_block, slot * CLS_DEV, CLS_DEV, 0)
    quarter = total // 4
    real_part = modulated[:, :half]
    imag_part = modulated[:, half:]
    freq = jnp.arange(half, dtype=jnp.int32) % MFREQ
    variants = []
    for u in range(4):
        step = (freq * u) % 4
        re_u = jnp.where(step == 0, real_part, jnp.where(step == 1, imag_part, jnp.where(step == 2, -real_part, -imag_part)))
        im_u = jnp.where(step == 0, imag_part, jnp.where(step == 1, -real_part, jnp.where(step == 2, -imag_part, real_part)))
        variants.append(jnp.concatenate([re_u, im_u], axis=1))
    stacked = jnp.concatenate(variants, axis=0)
    turned = rotate_all(refs_block.astype(jnp.float32), quarter, total)
    found = lax.dot_general(
        stacked, turned, (((1,), (1,)), ((), ())), preferred_element_type=jnp.float32
    )
    best = jnp.max(found.reshape(4, count, quarter, block), axis=(0, 2)) * (1.0 / math.sqrt(K))
    sent, best = lax.optimization_barrier((sent, best))
    refs = lax.ppermute(sent, ("dom", "rot"), pairs)
    best_scores = lax.all_to_all(best, "rot", 0, 1, tiled=True)

    return (refs, best_scores)


def solution(mesh):
    in_specs = (P("dom", None), P("dom"), P("dom"), P("dom"), P())
    out_specs = (P("dom", None), P(("dom", "rot"), None))
    return jax.shard_map(local, mesh=mesh, in_specs=in_specs, out_specs=out_specs, check_vma=False)
```

```python
import math

import jax
import numpy as np
import jax.numpy as jnp
from jax import lax
from jax.experimental import pallas as pl
from jax.experimental.pallas import tpu as pltpu
from jax.sharding import PartitionSpec as P

CYCLES = 64
MFREQ = 64
CLS_DEV = 6
K = 8192


def column_angles(index, total, width):
    freqs = lax.broadcasted_iota(jnp.int32, (index.shape[0], width), 1) % MFREQ
    phase = freqs * index[:, None] % total
    return phase.astype(jnp.float32) * (2.0 * math.pi / total)


def split_dot(member, value):
    high = value.astype(jnp.bfloat16)
    rest = value - high.astype(jnp.float32)
    mid = rest.astype(jnp.bfloat16)
    low = (rest - mid.astype(jnp.float32)).astype(jnp.bfloat16)
    total = jnp.dot(member, high, preferred_element_type=jnp.float32)
    total = total + jnp.dot(member, mid, preferred_element_type=jnp.float32)
    return total + jnp.dot(member, low, preferred_element_type=jnp.float32)


def prologue_kernel(
    x_ref, cos_ref, sin_ref, rot_ref, group_ref, table_ref, assign_ref,
    pay_ref, mod_ref, w_ref, ctf_ref, cos_scr, sin_scr,
):
    count = x_ref.shape[0]
    block = pay_ref.shape[1]
    for p in range(count):
        ctf_ref[pl.ds(p, 1), :] = table_ref[pl.ds(group_ref[p], 1), :]
        cos_scr[pl.ds(p, 1), :] = cos_ref[pl.ds(rot_ref[p], 1), :]
        sin_scr[pl.ds(p, 1), :] = sin_ref[pl.ds(rot_ref[p], 1), :]
    first_class = lax.axis_index("rot") * block
    classes = first_class + lax.broadcasted_iota(jnp.int32, (block, count), 0)
    member = (classes == assign_ref[...]).astype(jnp.bfloat16)
    half = x_ref.shape[1] // 2
    lanes = cos_ref.shape[1]
    chunks, _, width = pay_ref.shape
    width -= ctf_ref.shape[1]
    cosine = cos_scr[...]
    sine = sin_scr[...]
    low = lax.broadcasted_iota(jnp.int32, cosine.shape, 1) < MFREQ
    for j in range(half // lanes):
        gain = jnp.where(low, ctf_ref[:, 2 * j : 2 * j + 1], ctf_ref[:, 2 * j + 1 : 2 * j + 2])
        re_cols = pl.ds(j * lanes, lanes)
        im_cols = pl.ds(half + j * lanes, lanes)
        real_part = x_ref[:, re_cols].astype(jnp.float32)
        imag_part = x_ref[:, im_cols].astype(jnp.float32)
        w_ref[:, re_cols] = (real_part * cosine + imag_part * sine) * gain
        w_ref[:, im_cols] = (imag_part * cosine - real_part * sine) * gain
        mod_ref[:, re_cols] = (real_part * gain).astype(jnp.bfloat16)
        mod_ref[:, im_cols] = (imag_part * gain).astype(jnp.bfloat16)
    gains = ctf_ref[...]
    denom = split_dot(member, gains * gains)
    numer = split_dot(member, w_ref[...])
    for x in range(chunks):
        pay_ref[x, :, :width] = numer[:, x * width : (x + 1) * width]
        pay_ref[x, :, width:] = denom


def derotate_and_sum(particles, rotation, group, ctf_table, assign, block, chunks, total):
    phase = (np.arange(2 * MFREQ)[None, :] % MFREQ) * np.arange(total)[:, None] % total
    angle = phase.astype(np.float32) * np.float32(2.0 * math.pi / total)
    count = particles.shape[0]
    smem = pl.BlockSpec(memory_space=pltpu.SMEM)
    vmem = pl.BlockSpec(memory_space=pltpu.VMEM)
    return pl.pallas_call(
        prologue_kernel,
        out_shape=(
            jax.ShapeDtypeStruct((chunks, block, K // chunks + CYCLES), jnp.float32),
            jax.ShapeDtypeStruct((count, K), jnp.bfloat16),
        ),
        in_specs=[vmem, vmem, vmem, smem, smem, vmem, vmem],
        scratch_shapes=[
            pltpu.VMEM((count, K), jnp.float32),
            pltpu.VMEM((count, ctf_table.shape[1]), jnp.float32),
            pltpu.VMEM((count, 2 * MFREQ), jnp.float32),
            pltpu.VMEM((count, 2 * MFREQ), jnp.float32),
        ],
    )(
        particles,
        jnp.asarray(np.cos(angle)),
        jnp.asarray(np.sin(angle)),
        rotation,
        group,
        ctf_table,
        assign.reshape(1, count),
    )


def rotate_all(refs, turns, total):
    count = refs.shape[0]
    half = K // 2
    real_part = refs[None, :, :half]
    imag_part = refs[None, :, half:]
    angle = column_angles(jnp.arange(turns, dtype=jnp.int32), total, half)
    cosine = jnp.cos(angle)[:, None, :]
    sine = jnp.sin(angle)[:, None, :]
    turned = jnp.concatenate(
        [real_part * cosine - imag_part * sine, real_part * sine + imag_part * cosine], axis=2
    )
    return turned.reshape(turns * count, K).astype(jnp.bfloat16)


def local(particles, assign, rot_index, group, ctf_table):
    dom_rank = lax.axis_index("dom")
    rot_count = lax.axis_size("rot")
    rot_rank = lax.axis_index("rot")
    dom_count = lax.axis_size("dom")
    classes = CLS_DEV * dom_count
    block = classes // rot_count
    owners_per_block = block // CLS_DEV
    total = 8 * rot_count
    count = particles.shape[0]

    half = K // 2
    chunks = dom_count
    width = K // chunks
    per_chunk = width // MFREQ
    payload, modulated = derotate_and_sum(
        particles, rot_index, group, ctf_table, assign, block, chunks, total
    )
    summed = jnp.sum(lax.all_to_all(payload, "dom", 0, 0, tiled=True), axis=0)
    modulated, summed = lax.optimization_barrier((modulated, summed))
    numer_chunk = summed[:, :width].reshape(block, per_chunk, MFREQ)
    first_cycle = (dom_rank * per_chunk) % CYCLES
    denom_chunk = lax.dynamic_slice_in_dim(summed[:, width:], first_cycle, per_chunk, 1)
    plain_chunk = (numer_chunk / (denom_chunk[:, :, None] + 1.0)).reshape(block, width)
    plain = lax.all_to_all(
        jnp.broadcast_to(plain_chunk[None], (chunks, block, width)), "dom", 0, 0, tiled=True
    )
    plain = plain.transpose(1, 0, 2).reshape(block, K)
    spread = jnp.mean(plain * plain, axis=1)
    refs_f32 = plain / jnp.sqrt(spread + 1e-06)[:, None]
    refs_block = refs_f32.astype(jnp.bfloat16)

    others = rot_count - 1
    pairs = []
    for plane in range(rot_count):
        first_owner = plane * owners_per_block
        senders = [x for x in range(dom_count) if x // owners_per_block != plane]
        for owner in range(first_owner, first_owner + owners_per_block):
            pairs.append((owner * rot_count + plane, owner * rot_count + plane))
        for idx, sender in enumerate(senders[: owners_per_block * others]):
            owner = first_owner + idx // others
            target = (plane + 1 + idx % others) % rot_count
            pairs.append((sender * rot_count + plane, owner * rot_count + target))
    own_plane = (dom_rank // owners_per_block) == rot_rank
    idx = jnp.where(dom_rank > rot_rank * owners_per_block, dom_rank - owners_per_block, dom_rank)
    slot = jnp.where(own_plane, dom_rank % owners_per_block, jnp.minimum(idx // others, owners_per_block - 1))
    sent = lax.dynamic_slice_in_dim(refs_block, slot * CLS_DEV, CLS_DEV, 0)
    quarter = total // 4
    real_part = modulated[:, :half]
    imag_part = modulated[:, half:]
    freq = jnp.arange(half, dtype=jnp.int32) % MFREQ
    variants = []
    for u in range(4):
        step = (freq * u) % 4
        re_u = jnp.where(step == 0, real_part, jnp.where(step == 1, imag_part, jnp.where(step == 2, -real_part, -imag_part)))
        im_u = jnp.where(step == 0, imag_part, jnp.where(step == 1, -real_part, jnp.where(step == 2, -imag_part, real_part)))
        variants.append(jnp.concatenate([re_u, im_u], axis=1))
    stacked = jnp.concatenate(variants, axis=0)
    turned = rotate_all(refs_block.astype(jnp.float32), quarter, total)
    found = lax.dot_general(
        stacked, turned, (((1,), (1,)), ((), ())), preferred_element_type=jnp.float32
    )
    best = jnp.max(found.reshape(4, count, quarter, block), axis=(0, 2)) * (1.0 / math.sqrt(K))
    sent, best = lax.optimization_barrier((sent, best))
    refs = lax.ppermute(sent, ("dom", "rot"), pairs)
    best_scores = lax.all_to_all(best, "rot", 0, 1, tiled=True)

    return (refs, best_scores)


def solution(mesh):
    in_specs = (P("dom", None), P("dom"), P("dom"), P("dom"), P())
    out_specs = (P("dom", None), P(("dom", "rot"), None))
    return jax.shard_map(local, mesh=mesh, in_specs=in_specs, out_specs=out_specs, check_vma=False)
```

```python
import math

import jax
import numpy as np
import jax.numpy as jnp
from jax import lax
from jax.experimental import pallas as pl
from jax.experimental.pallas import tpu as pltpu
from jax.sharding import PartitionSpec as P

CYCLES = 64
MFREQ = 64
CLS_DEV = 6
K = 8192


def column_angles(index, total, width):
    freqs = lax.broadcasted_iota(jnp.int32, (index.shape[0], width), 1) % MFREQ
    phase = freqs * index[:, None] % total
    return phase.astype(jnp.float32) * (2.0 * math.pi / total)


def split_dot(member, value):
    high = value.astype(jnp.bfloat16)
    low = (value - high.astype(jnp.float32)).astype(jnp.bfloat16)
    total = jnp.dot(member, high, preferred_element_type=jnp.float32)
    return total + jnp.dot(member, low, preferred_element_type=jnp.float32)


def prologue_kernel(
    x_ref, cos_ref, sin_ref, rot_ref, group_ref, table_ref, assign_ref,
    pay_ref, mod_ref, w_ref, ctf_ref, cos_scr, sin_scr,
):
    count = x_ref.shape[0]
    block = pay_ref.shape[1]
    for p in range(count):
        ctf_ref[pl.ds(p, 1), :] = table_ref[pl.ds(group_ref[p], 1), :]
        cos_scr[pl.ds(p, 1), :] = cos_ref[pl.ds(rot_ref[p], 1), :]
        sin_scr[pl.ds(p, 1), :] = sin_ref[pl.ds(rot_ref[p], 1), :]
    first_class = lax.axis_index("rot") * block
    classes = first_class + lax.broadcasted_iota(jnp.int32, (block, count), 0)
    member = (classes == assign_ref[...]).astype(jnp.bfloat16)
    half = x_ref.shape[1] // 2
    lanes = cos_ref.shape[1]
    chunks, _, width = pay_ref.shape
    width -= ctf_ref.shape[1]
    cosine = cos_scr[...]
    sine = sin_scr[...]
    low = lax.broadcasted_iota(jnp.int32, cosine.shape, 1) < MFREQ
    for j in range(half // lanes):
        gain = jnp.where(low, ctf_ref[:, 2 * j : 2 * j + 1], ctf_ref[:, 2 * j + 1 : 2 * j + 2])
        re_cols = pl.ds(j * lanes, lanes)
        im_cols = pl.ds(half + j * lanes, lanes)
        real_part = x_ref[:, re_cols].astype(jnp.float32)
        imag_part = x_ref[:, im_cols].astype(jnp.float32)
        w_ref[:, re_cols] = (real_part * cosine + imag_part * sine) * gain
        w_ref[:, im_cols] = (imag_part * cosine - real_part * sine) * gain
        mod_ref[:, re_cols] = (real_part * gain).astype(jnp.bfloat16)
        mod_ref[:, im_cols] = (imag_part * gain).astype(jnp.bfloat16)
    gains = ctf_ref[...]
    denom = split_dot(member, gains * gains)
    numer = split_dot(member, w_ref[...])
    for x in range(chunks):
        pay_ref[x, :, :width] = numer[:, x * width : (x + 1) * width]
        pay_ref[x, :, width:] = denom


def derotate_and_sum(particles, rotation, group, ctf_table, assign, block, chunks, total):
    phase = (np.arange(2 * MFREQ)[None, :] % MFREQ) * np.arange(total)[:, None] % total
    angle = phase.astype(np.float32) * np.float32(2.0 * math.pi / total)
    count = particles.shape[0]
    smem = pl.BlockSpec(memory_space=pltpu.SMEM)
    vmem = pl.BlockSpec(memory_space=pltpu.VMEM)
    return pl.pallas_call(
        prologue_kernel,
        out_shape=(
            jax.ShapeDtypeStruct((chunks, block, K // chunks + CYCLES), jnp.float32),
            jax.ShapeDtypeStruct((count, K), jnp.bfloat16),
        ),
        in_specs=[vmem, vmem, vmem, smem, smem, vmem, vmem],
        scratch_shapes=[
            pltpu.VMEM((count, K), jnp.float32),
            pltpu.VMEM((count, ctf_table.shape[1]), jnp.float32),
            pltpu.VMEM((count, 2 * MFREQ), jnp.float32),
            pltpu.VMEM((count, 2 * MFREQ), jnp.float32),
        ],
    )(
        particles,
        jnp.asarray(np.cos(angle)),
        jnp.asarray(np.sin(angle)),
        rotation,
        group,
        ctf_table,
        assign.reshape(1, count),
    )


def rotate_all(refs, turns, total):
    count = refs.shape[0]
    half = K // 2
    real_part = refs[None, :, :half]
    imag_part = refs[None, :, half:]
    angle = column_angles(jnp.arange(turns, dtype=jnp.int32), total, half)
    cosine = jnp.cos(angle)[:, None, :]
    sine = jnp.sin(angle)[:, None, :]
    turned = jnp.concatenate(
        [real_part * cosine - imag_part * sine, real_part * sine + imag_part * cosine], axis=2
    )
    return turned.reshape(turns * count, K).astype(jnp.bfloat16)


def local(particles, assign, rot_index, group, ctf_table):
    dom_rank = lax.axis_index("dom")
    rot_count = lax.axis_size("rot")
    rot_rank = lax.axis_index("rot")
    dom_count = lax.axis_size("dom")
    classes = CLS_DEV * dom_count
    block = classes // rot_count
    owners_per_block = block // CLS_DEV
    total = 8 * rot_count
    count = particles.shape[0]

    half = K // 2
    chunks = dom_count
    width = K // chunks
    per_chunk = width // MFREQ
    payload, modulated = derotate_and_sum(
        particles, rot_index, group, ctf_table, assign, block, chunks, total
    )
    summed = jnp.sum(lax.all_to_all(payload, "dom", 0, 0, tiled=True), axis=0)
    numer_chunk = summed[:, :width].reshape(block, per_chunk, MFREQ)
    first_cycle = (dom_rank * per_chunk) % CYCLES
    denom_chunk = lax.dynamic_slice_in_dim(summed[:, width:], first_cycle, per_chunk, 1)
    plain_chunk = (numer_chunk / (denom_chunk[:, :, None] + 1.0)).reshape(block, width)
    plain = lax.all_to_all(
        jnp.broadcast_to(plain_chunk[None], (chunks, block, width)), "dom", 0, 0, tiled=True
    )
    plain = plain.transpose(1, 0, 2).reshape(block, K)
    spread = jnp.mean(plain * plain, axis=1)
    refs_f32 = plain / jnp.sqrt(spread + 1e-06)[:, None]
    refs_block = refs_f32.astype(jnp.bfloat16)

    others = rot_count - 1
    pairs = []
    for plane in range(rot_count):
        first_owner = plane * owners_per_block
        senders = [x for x in range(dom_count) if x // owners_per_block != plane]
        for owner in range(first_owner, first_owner + owners_per_block):
            pairs.append((owner * rot_count + plane, owner * rot_count + plane))
        for idx, sender in enumerate(senders[: owners_per_block * others]):
            owner = first_owner + idx // others
            target = (plane + 1 + idx % others) % rot_count
            pairs.append((sender * rot_count + plane, owner * rot_count + target))
    own_plane = (dom_rank // owners_per_block) == rot_rank
    idx = jnp.where(dom_rank > rot_rank * owners_per_block, dom_rank - owners_per_block, dom_rank)
    slot = jnp.where(own_plane, dom_rank % owners_per_block, jnp.minimum(idx // others, owners_per_block - 1))
    sent = lax.dynamic_slice_in_dim(refs_block, slot * CLS_DEV, CLS_DEV, 0)
    quarter = total // 4
    real_part = modulated[:, :half]
    imag_part = modulated[:, half:]
    freq = jnp.arange(half, dtype=jnp.int32) % MFREQ
    variants = []
    for u in range(4):
        step = (freq * u) % 4
        re_u = jnp.where(step == 0, real_part, jnp.where(step == 1, imag_part, jnp.where(step == 2, -real_part, -imag_part)))
        im_u = jnp.where(step == 0, imag_part, jnp.where(step == 1, -real_part, jnp.where(step == 2, -imag_part, real_part)))
        variants.append(jnp.concatenate([re_u, im_u], axis=1))
    stacked = jnp.concatenate(variants, axis=0)
    turned = rotate_all(refs_block.astype(jnp.float32), quarter, total)
    found = lax.dot_general(
        stacked, turned, (((1,), (1,)), ((), ())), preferred_element_type=jnp.float32
    )
    best = jnp.max(found.reshape(4, count, quarter, block), axis=(0, 2)) * (1.0 / math.sqrt(K))
    sent, best = lax.optimization_barrier((sent, best))
    refs = lax.ppermute(sent, ("dom", "rot"), pairs)
    best_scores = lax.all_to_all(best, "rot", 0, 1, tiled=True)

    return (refs, best_scores)


def solution(mesh):
    in_specs = (P("dom", None), P("dom"), P("dom"), P("dom"), P())
    out_specs = (P("dom", None), P(("dom", "rot"), None))
    return jax.shard_map(local, mesh=mesh, in_specs=in_specs, out_specs=out_specs, check_vma=False)
```
